32 devices in a mesh: groups: 2 (over y), feat: 4 (over z), tower: 4 (over x, core).
Axes of the slice: x: 2, y: 2, z: 4, core: 2. Of those that a mesh axis runs over, the one named last changes fastest.
Arguments:
- pooled_first: bfloat16 [4, 16, 3072, 128], P('tower', 'feat', 'groups'), parts along dimension 2, may hold values from -6 to 6
- pooled_second: bfloat16 [4, 16, 3072, 128], P('tower', 'feat', 'groups'), parts along dimension 2, may hold values from -6 to 6
- feature_order: int32 [4, 32], P('tower'), may hold values from 0 to 31, each once within a row
- cross_down: bfloat16 [4, 4096, 256], P('tower', 'feat'), may hold values from -0.09375 to 0.09375
- cross_up: bfloat16 [4, 4096, 256], P('tower', 'feat'), may hold values from -0.375 to 0.375
- cross_bias: float32 [4, 4096], P('tower'), may hold values from -3 to 3
- compress_weight: bfloat16 [4, 4096, 512], P('tower', 'feat'), may hold values from -0.09375 to 0.09375
- compress_bias: float32 [4, 512], P('tower'), may hold values from -3 to 3
- dense_vector: bfloat16 [3072, 128], P(('groups', 'feat', 'tower')), parts along dimension 0, may hold values from -6 to 6
- mlp_weight: bfloat16 [248, 1024], P('tower'), may hold values from -0.375 to 0.375
- mlp_bias: float32 [1024], replicated, may hold values from -3 to 3
Outputs:
- top_hidden: bfloat16 [3072, 1024], P(('groups', 'feat', 'tower')), parts along dimension 0
The draws below stay inside these ranges and needn't reach their ends.
There are 2 independent parts, one for each index of `groups`. The reference program is written for one: setup_inputs(seed, part) draws one part's arguments, and reference() takes and returns one part's arrays. A program takes and returns all parts, laid end to end along the dimension named above; an argument that names none is the same for every part. Nothing has to cross between parts.
Inputs may be any that keep to these rules, and one draw needn't show every extreme that they name: Each row of feature_order names every number from 0 to 31 once.
All inputs are finite; a program needn't handle non-finite values.
Results may differ from the reference program's by a relative error of at most 0.0072.
Values may be sent and summed in bfloat16 or wider, within the bound.
No kernel may reach another device: no remote copies, remote signals or barrier semaphores. Data moves between devices by JAX's collectives and lax.ppermute only.
A program may use at most 64 MiB of HBM per device.

```python
import math
import jax
import jax.numpy as jnp
import numpy as np
from jax import lax

E = 128
FG = 16
K = 256
DENSE = 128
HID = 1024
FPT = 32
W = 4096
P_SIZE = 512
TOWERS = 4
NV = 16
IN = 248
BATCH = 1536


def shard_levels(key, extent, shards, smallest, top_value):
    factor_of, own = 1.0, jax.random.fold_in(key, 6)
    for position, blocks in shards:
        steps = jnp.exp(jax.random.uniform(jax.random.fold_in(own, position), (blocks,), jnp.float32, smallest / len(shards), top_value / len(shards)))
        factor_of = factor_of * jnp.repeat(steps, extent[position] // blocks).reshape([-1 if axis == position else 1 for axis in range(len(extent))])
    return factor_of


def bell_draw(stream_key, dims, spread, most, shards=(), kind=jnp.bfloat16):
    gain = shard_levels(stream_key, dims, shards, -0.22, 0.18) if shards else 1.0
    drawn = jax.random.normal(stream_key, dims, jnp.float32) * spread * gain
    return jnp.minimum(jnp.maximum(drawn, -most), most).astype(kind)


def setup_inputs(seed: int = 0, part: int = 0) -> dict:
    key_of = jax.random.split(jax.random.key(seed), 12)
    part_keys = jax.random.split(jax.random.fold_in(key_of[11], part), 12)
    pooled_first = bell_draw(part_keys[0], (TOWERS, FG, BATCH, E), 1.0, 6.0, ((0, 4), (1, 4)))
    pooled_second = bell_draw(part_keys[1], (TOWERS, FG, BATCH, E), 1.0, 6.0, ((0, 4), (1, 4)))
    feature_order = jax.vmap(lambda own: jax.random.permutation(own, FPT))(jax.random.split(key_of[2], TOWERS)).reshape((TOWERS, FPT)).astype(jnp.int32)
    cross_down = bell_draw(key_of[3], (TOWERS, W, K), W ** -0.5, 0.09375, ((0, 4), (1, 4)))
    cross_up = bell_draw(key_of[4], (TOWERS, W, K), K ** -0.5, 0.375, ((0, 4), (1, 4)))
    cross_bias = bell_draw(key_of[5], (TOWERS, W), 0.5, 3.0, ((0, 4),), jnp.float32)
    compress_weight = bell_draw(key_of[6], (TOWERS, W, P_SIZE), W ** -0.5, 0.09375, ((0, 4), (1, 4)))
    compress_bias = bell_draw(key_of[7], (TOWERS, P_SIZE), 0.5, 3.0, ((0, 4),), jnp.float32)
    dense_vector = bell_draw(part_keys[8], (BATCH, DENSE), 1.0, 6.0, ((0, 16),))
    mlp_weight = bell_draw(key_of[9], (IN, HID), IN ** -0.5, 0.375, ((0, 4),))
    mlp_bias = bell_draw(key_of[10], (HID,), 0.5, 3.0, (), jnp.float32)
    return dict(pooled_first=pooled_first, pooled_second=pooled_second, feature_order=feature_order, cross_down=cross_down, cross_up=cross_up, cross_bias=cross_bias, compress_weight=compress_weight, compress_bias=compress_bias, dense_vector=dense_vector, mlp_weight=mlp_weight, mlp_bias=mlp_bias)


def tower_step(tower_args):
    group_one, group_two, orders, down_rows, up_rows, cross_shift, squeeze_rows, squeeze_bias = tower_args
    slot_data = jnp.concatenate([group_one, group_two], 0).astype(jnp.float32)
    one_hot = (orders[None, :] == jnp.arange(FPT, dtype=jnp.int32)[:, None]).astype(jnp.float32)
    base_rows = jnp.einsum('fs,sre->rfe', one_hot, slot_data).astype(jnp.bfloat16).reshape(BATCH, W)
    low_rank = jnp.dot(base_rows, down_rows, preferred_element_type=jnp.float32).astype(jnp.bfloat16)
    lifted = lax.dot_general(low_rank, up_rows, (((1,), (1,)), ((), ())), preferred_element_type=jnp.float32)
    base_float = base_rows.astype(jnp.float32)
    crossed = (base_float * (lifted + cross_shift[None, :]) + base_float).astype(jnp.bfloat16)
    return (jnp.dot(crossed, squeeze_rows, preferred_element_type=jnp.float32) + squeeze_bias[None, :]).astype(jnp.bfloat16)

def reference(pooled_first, pooled_second, feature_order, cross_down, cross_up, cross_bias, compress_weight, compress_bias, dense_vector, mlp_weight, mlp_bias):
    compressed = lax.map(tower_step, (pooled_first, pooled_second, feature_order, cross_down, cross_up, cross_bias, compress_weight, compress_bias))
    vectors = jnp.transpose(compressed, (1, 0, 2)).reshape(BATCH, NV, E).astype(jnp.float32)
    gram_matrix = jnp.einsum('bie,bje->bij', vectors, vectors) * (1.0 / math.sqrt(E))
    upper_rows, upper_cols = np.triu_indices(NV, 1)
    pair_index = upper_rows * NV + upper_cols
    pair_terms = gram_matrix.reshape(BATCH, NV * NV)[:, pair_index]
    joined = jnp.concatenate([dense_vector.astype(jnp.float32), pair_terms], 1).astype(jnp.bfloat16)
    hidden_sum = jnp.dot(joined, mlp_weight, preferred_element_type=jnp.float32) + mlp_bias[None, :]
    return jax.nn.relu(hidden_sum).astype(jnp.bfloat16)
```

```python
import functools
import math

import jax
import jax.numpy as jnp
import numpy as np
from jax import lax
from jax.sharding import PartitionSpec as P


def pair_positions(vector_count):
    upper_rows, upper_cols = np.triu_indices(vector_count, 1)
    return upper_rows * vector_count + upper_cols


def gathered_feature_order(rows_here, feat_count, group_count, entry_count):
    piece = rows_here // group_count
    positions = []
    for group in range(group_count):
        for owner in range(feat_count):
            start = owner * rows_here + group * piece
            positions.extend(range(start // entry_count, (start + piece) // entry_count))
    return np.asarray(positions, np.int32)


def on_device(
    pooled_first,
    pooled_second,
    feature_order,
    cross_down,
    cross_up,
    cross_bias,
    compress_weight,
    compress_bias,
    dense_vector,
    mlp_weight,
    mlp_bias,
    *,
    feat_count,
    group_count,
):
    entry_count = pooled_first.shape[3]
    rows_here = cross_down.shape[1]
    rank = cross_down.shape[2]
    split = rows_here % group_count == 0 and (rows_here // group_count) % entry_count == 0
    gather_groups = group_count if split else 1
    piece = rows_here // gather_groups

    hidden_weight = lax.all_gather(mlp_weight, "tower", axis=0, tiled=True)
    hidden_weight, pooled_first, pooled_second = lax.optimization_barrier(
        (hidden_weight, pooled_first, pooled_second)
    )

    weights_here = jnp.concatenate([cross_down[0], cross_up[0], compress_weight[0]], axis=1)
    if split:
        group_index = lax.axis_index("groups")
        weights_here = lax.dynamic_slice_in_dim(weights_here, group_index * piece, piece, axis=0)
        weights = lax.all_gather(weights_here, ("groups", "feat"), axis=0, tiled=True)
    else:
        weights = lax.all_gather(weights_here, "feat", axis=0, tiled=True)
    position_feature = gathered_feature_order(rows_here, feat_count, gather_groups, entry_count)

    group_one, group_two = (
        lax.all_to_all(pooled_first, "feat", split_axis=2, concat_axis=1, tiled=True),
        lax.all_to_all(pooled_second, "feat", split_axis=2, concat_axis=1, tiled=True),
    )
    slot_data = jnp.concatenate([group_one[0], group_two[0]], 0)
    slot_count = slot_data.shape[0]
    row_count = slot_data.shape[1]
    orders = feature_order[0]
    one_hot = (orders[None, :] == jnp.asarray(position_feature)[:, None]).astype(jnp.bfloat16)
    base_rows = jnp.einsum("fs,sre->rfe", one_hot, slot_data, preferred_element_type=jnp.float32)
    base_rows = base_rows.astype(jnp.bfloat16).reshape(row_count, slot_count * entry_count)

    width = slot_count * entry_count
    shift_row = cross_bias[0].reshape(width // entry_count, entry_count)[position_feature].reshape(width)
    down_piece = weights[:, :rank]
    up_piece = weights[:, rank : 2 * rank]
    squeeze_piece = weights[:, 2 * rank :]

    low_sum = jnp.dot(base_rows, down_piece, preferred_element_type=jnp.float32)
    low_rank = low_sum.astype(jnp.bfloat16)
    lifted = lax.dot_general(
        low_rank, up_piece, (((1,), (1,)), ((), ())), preferred_element_type=jnp.float32
    )
    columns = base_rows.astype(jnp.float32)
    crossed = (columns * (lifted + shift_row[None, :]) + columns).astype(jnp.bfloat16)
    squeezed = jnp.dot(crossed, squeeze_piece, preferred_element_type=jnp.float32)
    compressed = (squeezed + compress_bias[0][None, :]).astype(jnp.bfloat16)
    gathered = lax.all_to_all(compressed, "tower", split_axis=0, concat_axis=1, tiled=True)
    local_rows = gathered.shape[0]
    vector_count = gathered.shape[1] // entry_count
    vectors = gathered.reshape(local_rows, vector_count, entry_count)
    gram_matrix = jnp.einsum(
        "bie,bje->bij", vectors, vectors, preferred_element_type=jnp.float32
    ) * (1.0 / math.sqrt(entry_count))
    pair_terms = gram_matrix.reshape(local_rows, vector_count * vector_count)[
        :, pair_positions(vector_count)
    ]
    joined = jnp.concatenate([dense_vector.astype(jnp.float32), pair_terms], 1).astype(jnp.bfloat16)
    hidden_units = mlp_weight.shape[1]
    width_here = hidden_weight.shape[0]
    columns = lax.slice_in_dim(joined, 0, width_here, axis=1)
    hidden_sum = jnp.zeros((local_rows, hidden_units), jnp.float32) + jnp.dot(
        columns, hidden_weight, preferred_element_type=jnp.float32
    )
    return jax.nn.relu(hidden_sum + mlp_bias[None, :]).astype(jnp.bfloat16)


def solution(mesh):
    in_specs = (
        P("tower", "feat", "groups", None),
        P("tower", "feat", "groups", None),
        P("tower", None),
        P("tower", "feat", None),
        P("tower", "feat", None),
        P("tower", None),
        P("tower", "feat", None),
        P("tower", None),
        P(("groups", "feat", "tower"), None),
        P("tower", None),
        P(),
    )
    out_specs = P(("groups", "feat", "tower"), None)
    body = functools.partial(
        on_device, feat_count=mesh.shape["feat"], group_count=mesh.shape["groups"]
    )
    return jax.shard_map(body, mesh=mesh, in_specs=in_specs, out_specs=out_specs, check_vma=False)
```

```python
import functools
import math

import jax
import jax.numpy as jnp
import numpy as np
from jax import lax
from jax.sharding import PartitionSpec as P


def pair_positions(vector_count):
    upper_rows, upper_cols = np.triu_indices(vector_count, 1)
    return upper_rows * vector_count + upper_cols


def received_feature_table(rows_here, feat_count, group_count, entry_count):
    piece = rows_here // group_count
    table = np.zeros((group_count, group_count, feat_count * piece // entry_count), np.int32)
    for group in range(group_count):
        for shift in range(group_count):
            source = (group - shift) % group_count
            blocks = []
            for owner in range(feat_count):
                start = owner * rows_here + source * piece
                blocks.extend(range(start // entry_count, (start + piece) // entry_count))
            table[group, shift] = blocks
    return table


def gather_rows(part, group_count):
    own = lax.all_gather(part, "feat", axis=0, tiled=True)
    received = [own]
    for shift in range(1, group_count):
        pairs = [(source, (source + shift) % group_count) for source in range(group_count)]
        received.append(lax.ppermute(own, "groups", pairs))
    return received


def on_device(
    pooled_first,
    pooled_second,
    feature_order,
    cross_down,
    cross_up,
    cross_bias,
    compress_weight,
    compress_bias,
    dense_vector,
    mlp_weight,
    mlp_bias,
    *,
    feat_count,
    group_count,
):
    entry_count = pooled_first.shape[3]
    rows_here = cross_down.shape[1]
    rank = cross_down.shape[2]
    split = rows_here % group_count == 0 and (rows_here // group_count) % entry_count == 0
    share_count = group_count if split else 1
    piece = rows_here // share_count

    first_here = jnp.concatenate([cross_down[0], cross_up[0]], axis=1)
    second_here = compress_weight[0]
    if split:
        group_index = lax.axis_index("groups")
        first_here = lax.dynamic_slice_in_dim(first_here, group_index * piece, piece, axis=0)
        second_here = lax.dynamic_slice_in_dim(second_here, group_index * piece, piece, axis=0)
        table = jnp.asarray(received_feature_table(rows_here, feat_count, share_count, entry_count))
        position_feature = table[group_index]
    else:
        position_feature = jnp.asarray(
            received_feature_table(rows_here, feat_count, 1, entry_count)
        )[0]
    first_parts = gather_rows(first_here, share_count)
    second_parts = gather_rows(second_here, share_count)

    group_one, group_two = (
        lax.all_to_all(pooled_first, "feat", split_axis=2, concat_axis=1, tiled=True),
        lax.all_to_all(pooled_second, "feat", split_axis=2, concat_axis=1, tiled=True),
    )
    mlp_weight, group_one = lax.optimization_barrier((mlp_weight, group_one))
    hidden_weight = lax.all_gather(mlp_weight, "tower", axis=0, tiled=True)

    slot_data = jnp.concatenate([group_one[0], group_two[0]], 0)
    slot_count = slot_data.shape[0]
    row_count = slot_data.shape[1]
    orders = feature_order[0]
    position_count = position_feature.shape[1]
    one_hot = (orders[None, None, :] == position_feature[:, :, None]).astype(jnp.bfloat16)
    base_parts = jnp.einsum("kfs,sre->krfe", one_hot, slot_data, preferred_element_type=jnp.float32)
    base_parts = base_parts.astype(jnp.bfloat16).reshape(
        share_count, row_count, position_count * entry_count
    )
    bias_blocks = cross_bias[0].reshape(slot_count, entry_count)

    low_sum = None
    for shift in range(share_count):
        term = jnp.dot(
            base_parts[shift], first_parts[shift][:, :rank], preferred_element_type=jnp.float32
        )
        low_sum = term if low_sum is None else low_sum + term
    low_rank = low_sum.astype(jnp.bfloat16)

    squeezed = None
    for shift in range(share_count):
        lifted = lax.dot_general(
            low_rank,
            first_parts[shift][:, rank:],
            (((1,), (1,)), ((), ())),
            preferred_element_type=jnp.float32,
        )
        shift_row = bias_blocks[position_feature[shift]].reshape(position_count * entry_count)
        columns = base_parts[shift].astype(jnp.float32)
        crossed = (columns * (lifted + shift_row[None, :]) + columns).astype(jnp.bfloat16)
        term = jnp.dot(crossed, second_parts[shift], preferred_element_type=jnp.float32)
        squeezed = term if squeezed is None else squeezed + term
    compressed = (squeezed + compress_bias[0][None, :]).astype(jnp.bfloat16)
    gathered = lax.all_to_all(compressed, "tower", split_axis=0, concat_axis=1, tiled=True)
    local_rows = gathered.shape[0]
    vector_count = gathered.shape[1] // entry_count
    vectors = gathered.reshape(local_rows, vector_count, entry_count)
    gram_matrix = jnp.einsum(
        "bie,bje->bij", vectors, vectors, preferred_element_type=jnp.float32
    ) * (1.0 / math.sqrt(entry_count))
    pair_terms = gram_matrix.reshape(local_rows, vector_count * vector_count)[
        :, pair_positions(vector_count)
    ]
    joined = jnp.concatenate([dense_vector.astype(jnp.float32), pair_terms], 1).astype(jnp.bfloat16)
    hidden_units = mlp_weight.shape[1]
    width_here = hidden_weight.shape[0]
    columns = lax.slice_in_dim(joined, 0, width_here, axis=1)
    hidden_sum = jnp.zeros((local_rows, hidden_units), jnp.float32) + jnp.dot(
        columns, hidden_weight, preferred_element_type=jnp.float32
    )
    return jax.nn.relu(hidden_sum + mlp_bias[None, :]).astype(jnp.bfloat16)


def solution(mesh):
    in_specs = (
        P("tower", "feat", "groups", None),
        P("tower", "feat", "groups", None),
        P("tower", None),
        P("tower", "feat", None),
        P("tower", "feat", None),
        P("tower", None),
        P("tower", "feat", None),
        P("tower", None),
        P(("groups", "feat", "tower"), None),
        P("tower", None),
        P(),
    )
    out_specs = P(("groups", "feat", "tower"), None)
    body = functools.partial(
        on_device, feat_count=mesh.shape["feat"], group_count=mesh.shape["groups"]
    )
    return jax.shard_map(body, mesh=mesh, in_specs=in_specs, out_specs=out_specs, check_vma=False)
```

```python
import functools
import math

import jax
import jax.numpy as jnp
import numpy as np
from jax import lax
from jax.sharding import PartitionSpec as P


def pair_positions(vector_count):
    upper_rows, upper_cols = np.triu_indices(vector_count, 1)
    return upper_rows * vector_count + upper_cols


def weight_parts(weights_here, feat_count, group_count, share_count, entry_count):
    rows_here = weights_here.shape[0]
    piece = rows_here // share_count
    blocks_here = rows_here // entry_count
    blocks_piece = piece // entry_count
    owner = lax.axis_index("feat")
    group = lax.axis_index("groups") if share_count > 1 else 0
    block_range = jnp.arange(blocks_piece, dtype=jnp.int32)
    parts = [(weights_here, owner * blocks_here + jnp.arange(blocks_here, dtype=jnp.int32))]
    if share_count > 1:
        travelling = lax.dynamic_slice_in_dim(weights_here, group * piece, piece, axis=0)
    else:
        travelling = weights_here
    ring = [(source, (source + 1) % feat_count) for source in range(feat_count)]
    for step in range(1, feat_count):
        travelling = lax.ppermute(travelling, "feat", ring)
        source_block = (owner - step) % feat_count
        parts.append(
            (travelling, source_block * blocks_here + group * blocks_piece + block_range)
        )
        for shift in range(1, share_count):
            pairs = [(source, (source + shift) % group_count) for source in range(group_count)]
            forwarded = lax.ppermute(travelling, "groups", pairs)
            from_group = (group - shift) % group_count
            parts.append(
                (forwarded, source_block * blocks_here + from_group * blocks_piece + block_range)
            )
    return parts


def on_device(
    pooled_first,
    pooled_second,
    feature_order,
    cross_down,
    cross_up,
    cross_bias,
    compress_weight,
    compress_bias,
    dense_vector,
    mlp_weight,
    mlp_bias,
    *,
    feat_count,
    group_count,
):
    entry_count = pooled_first.shape[3]
    rows_here = cross_down.shape[1]
    rank = cross_down.shape[2]
    split = rows_here % group_count == 0 and (rows_here // group_count) % entry_count == 0
    share_count = group_count if split else 1

    weights_here = jnp.concatenate([cross_down[0], cross_up[0], compress_weight[0]], axis=1)
    parts = weight_parts(weights_here, feat_count, group_count, share_count, entry_count)

    group_one, group_two = (
        lax.all_to_all(pooled_first, "feat", split_axis=2, concat_axis=1, tiled=True),
        lax.all_to_all(pooled_second, "feat", split_axis=2, concat_axis=1, tiled=True),
    )
    mlp_weight, group_one = lax.optimization_barrier((mlp_weight, group_one))
    hidden_weight = lax.all_gather(mlp_weight, "tower", axis=0, tiled=True)

    slot_data = jnp.concatenate([group_one[0], group_two[0]], 0)
    slot_count = slot_data.shape[0]
    row_count = slot_data.shape[1]
    orders = feature_order[0]
    bias_blocks = cross_bias[0].reshape(slot_count, entry_count)

    bases = []
    low_sum = None
    for rows, features in parts:
        one_hot = (orders[None, :] == features[:, None]).astype(jnp.bfloat16)
        base = jnp.einsum("fs,sre->rfe", one_hot, slot_data, preferred_element_type=jnp.float32)
        base = base.astype(jnp.bfloat16).reshape(row_count, features.shape[0] * entry_count)
        bases.append(base)
        term = jnp.dot(base, rows[:, :rank], preferred_element_type=jnp.float32)
        low_sum = term if low_sum is None else low_sum + term
    low_rank = low_sum.astype(jnp.bfloat16)

    squeezed = None
    for (rows, features), base in zip(parts, bases):
        lifted = lax.dot_general(
            low_rank,
            rows[:, rank : 2 * rank],
            (((1,), (1,)), ((), ())),
            preferred_element_type=jnp.float32,
        )
        shift_row = bias_blocks[features].reshape(features.shape[0] * entry_count)
        columns = base.astype(jnp.float32)
        crossed = (columns * (lifted + shift_row[None, :]) + columns).astype(jnp.bfloat16)
        term = jnp.dot(crossed, rows[:, 2 * rank :], preferred_element_type=jnp.float32)
        squeezed = term if squeezed is None else squeezed + term
    compressed = (squeezed + compress_bias[0][None, :]).astype(jnp.bfloat16)
    gathered = lax.all_to_all(compressed, "tower", split_axis=0, concat_axis=1, tiled=True)
    local_rows = gathered.shape[0]
    vector_count = gathered.shape[1] // entry_count
    vectors = gathered.reshape(local_rows, vector_count, entry_count)
    gram_matrix = jnp.einsum(
        "bie,bje->bij", vectors, vectors, preferred_element_type=jnp.float32
    ) * (1.0 / math.sqrt(entry_count))
    pair_terms = gram_matrix.reshape(local_rows, vector_count * vector_count)[
        :, pair_positions(vector_count)
    ]
    joined = jnp.concatenate([dense_vector.astype(jnp.float32), pair_terms], 1).astype(jnp.bfloat16)
    hidden_units = mlp_weight.shape[1]
    width_here = hidden_weight.shape[0]
    columns = lax.slice_in_dim(joined, 0, width_here, axis=1)
    hidden_sum = jnp.zeros((local_rows, hidden_units), jnp.float32) + jnp.dot(
        columns, hidden_weight, preferred_element_type=jnp.float32
    )
    return jax.nn.relu(hidden_sum + mlp_bias[None, :]).astype(jnp.bfloat16)


def solution(mesh):
    in_specs = (
        P("tower", "feat", "groups", None),
        P("tower", "feat", "groups", None),
        P("tower", None),
        P("tower", "feat", None),
        P("tower", "feat", None),
        P("tower", None),
        P("tower", "feat", None),
        P("tower", None),
        P(("groups", "feat", "tower"), None),
        P("tower", None),
        P(),
    )
    out_specs = P(("groups", "feat", "tower"), None)
    body = functools.partial(
        on_device, feat_count=mesh.shape["feat"], group_count=mesh.shape["groups"]
    )
    return jax.shard_map(body, mesh=mesh, in_specs=in_specs, out_specs=out_specs, check_vma=False)
```

```python
import functools
import math

import jax
import jax.numpy as jnp
import numpy as np
from jax import lax
from jax.sharding import PartitionSpec as P


def pair_positions(vector_count):
    upper_rows, upper_cols = np.triu_indices(vector_count, 1)
    return upper_rows * vector_count + upper_cols


def weight_parts(weights_here, feat_count, group_count, share_count, entry_count):
    rows_here = weights_here.shape[0]
    piece = rows_here // share_count
    blocks_here = rows_here // entry_count
    blocks_piece = piece // entry_count
    owner = lax.axis_index("feat")
    group = lax.axis_index("groups") if share_count > 1 else 0
    block_range = jnp.arange(blocks_piece, dtype=jnp.int32)
    parts = [(weights_here, owner * blocks_here + jnp.arange(blocks_here, dtype=jnp.int32))]
    if share_count > 1:
        travelling = lax.dynamic_slice_in_dim(weights_here, group * piece, piece, axis=0)
    else:
        travelling = weights_here
    ring = [(source, (source + 1) % feat_count) for source in range(feat_count)]
    for step in range(1, feat_count):
        travelling = lax.ppermute(travelling, "feat", ring)
        source_block = (owner - step) % feat_count
        parts.append(
            (travelling, source_block * blocks_here + group * blocks_piece + block_range)
        )
        for shift in range(1, share_count):
            pairs = [(source, (source + shift) % group_count) for source in range(group_count)]
            forwarded = lax.ppermute(travelling, "groups", pairs)
            from_group = (group - shift) % group_count
            parts.append(
                (forwarded, source_block * blocks_here + from_group * blocks_piece + block_range)
            )
    return parts


def exchange_rows(first, second, feat_count):
    slots_here, row_count, _ = first.shape
    share = row_count // feat_count
    owner = lax.axis_index("feat")
    pieces, ids = [], []
    for shift in range(feat_count):
        target = (owner + shift) % feat_count
        piece = jnp.concatenate(
            [
                lax.dynamic_slice_in_dim(first, target * share, share, axis=1),
                lax.dynamic_slice_in_dim(second, target * share, share, axis=1),
            ],
            0,
        )
        if shift:
            piece = lax.ppermute(
                piece, "feat", [(source, (source + shift) % feat_count) for source in range(feat_count)]
            )
        source = (owner - shift) % feat_count
        local = jnp.arange(slots_here, dtype=jnp.int32)
        ids.append(
            jnp.concatenate([source * slots_here + local, (feat_count + source) * slots_here + local])
        )
        pieces.append(piece)
    return jnp.concatenate(pieces, 0), jnp.concatenate(ids)


def on_device(
    pooled_first,
    pooled_second,
    feature_order,
    cross_down,
    cross_up,
    cross_bias,
    compress_weight,
    compress_bias,
    dense_vector,
    mlp_weight,
    mlp_bias,
    *,
    feat_count,
    group_count,
    tower_count,
):
    entry_count = pooled_first.shape[3]
    rows_here = cross_down.shape[1]
    rank = cross_down.shape[2]
    split = rows_here % group_count == 0 and (rows_here // group_count) % entry_count == 0
    share_count = group_count if split else 1

    hidden_pieces = [mlp_weight]
    for shift in range(1, tower_count):
        pairs = [(source, (source + shift) % tower_count) for source in range(tower_count)]
        hidden_pieces.append(lax.ppermute(mlp_weight, "tower", pairs))

    weights_here = jnp.concatenate([cross_down[0], cross_up[0], compress_weight[0]], axis=1)
    parts = weight_parts(weights_here, feat_count, group_count, share_count, entry_count)

    slot_data, slot_ids = exchange_rows(pooled_first[0], pooled_second[0], feat_count)
    slot_count = slot_data.shape[0]
    row_count = slot_data.shape[1]
    orders = feature_order[0][slot_ids]
    bias_blocks = cross_bias[0].reshape(slot_count, entry_count)

    bases = []
    low_sum = None
    for rows, features in parts:
        one_hot = (orders[None, :] == features[:, None]).astype(jnp.bfloat16)
        base = jnp.einsum("fs,sre->rfe", one_hot, slot_data, preferred_element_type=jnp.float32)
        base = base.astype(jnp.bfloat16).reshape(row_count, features.shape[0] * entry_count)
        bases.append(base)
        term = jnp.dot(base, rows[:, :rank], preferred_element_type=jnp.float32)
        low_sum = term if low_sum is None else low_sum + term
    low_rank = low_sum.astype(jnp.bfloat16)

    squeezed = None
    for (rows, features), base in zip(parts, bases):
        lifted = lax.dot_general(
            low_rank,
            rows[:, rank : 2 * rank],
            (((1,), (1,)), ((), ())),
            preferred_element_type=jnp.float32,
        )
        shift_row = bias_blocks[features].reshape(features.shape[0] * entry_count)
        columns = base.astype(jnp.float32)
        crossed = (columns * (lifted + shift_row[None, :]) + columns).astype(jnp.bfloat16)
        term = jnp.dot(crossed, rows[:, 2 * rank :], preferred_element_type=jnp.float32)
        squeezed = term if squeezed is None else squeezed + term
    compressed = (squeezed + compress_bias[0][None, :]).astype(jnp.bfloat16)
    gathered = lax.all_to_all(compressed, "tower", split_axis=0, concat_axis=1, tiled=True)
    local_rows = gathered.shape[0]
    vector_count = gathered.shape[1] // entry_count
    vectors = gathered.reshape(local_rows, vector_count, entry_count)
    gram_matrix = jnp.einsum(
        "bie,bje->bij", vectors, vectors, preferred_element_type=jnp.float32
    ) * (1.0 / math.sqrt(entry_count))
    pair_terms = gram_matrix.reshape(local_rows, vector_count * vector_count)[
        :, pair_positions(vector_count)
    ]
    joined = jnp.concatenate([dense_vector.astype(jnp.float32), pair_terms], 1).astype(jnp.bfloat16)
    hidden_units = mlp_weight.shape[1]
    hidden_rows = mlp_weight.shape[0]
    tower = lax.axis_index("tower")
    hidden_sum = jnp.zeros((local_rows, hidden_units), jnp.float32)
    for shift, rows in enumerate(hidden_pieces):
        source = (tower - shift) % tower_count
        columns = lax.dynamic_slice_in_dim(joined, source * hidden_rows, hidden_rows, axis=1)
        hidden_sum = hidden_sum + jnp.dot(columns, rows, preferred_element_type=jnp.float32)
    return jax.nn.relu(hidden_sum + mlp_bias[None, :]).astype(jnp.bfloat16)


def solution(mesh):
    in_specs = (
        P("tower", "feat", "groups", None),
        P("tower", "feat", "groups", None),
        P("tower", None),
        P("tower", "feat", None),
        P("tower", "feat", None),
        P("tower", None),
        P("tower", "feat", None),
        P("tower", None),
        P(("groups", "feat", "tower"), None),
        P("tower", None),
        P(),
    )
    out_specs = P(("groups", "feat", "tower"), None)
    body = functools.partial(
        on_device, feat_count=mesh.shape["feat"],
        group_count=mesh.shape["groups"],
        tower_count=mesh.shape["tower"],
    )
    return jax.shard_map(body, mesh=mesh, in_specs=in_specs, out_specs=out_specs, check_vma=False)
```

```python
import functools
import math

import jax
import jax.numpy as jnp
import numpy as np
from jax import lax
from jax.sharding import PartitionSpec as P


def pair_positions(vector_count):
    upper_rows, upper_cols = np.triu_indices(vector_count, 1)
    return upper_rows * vector_count + upper_cols


def weight_parts(weights_here, feat_count, group_count, share_count, entry_count):
    rows_here = weights_here.shape[0]
    piece = rows_here // share_count
    blocks_here = rows_here // entry_count
    blocks_piece = piece // entry_count
    owner = lax.axis_index("feat")
    group = lax.axis_index("groups") if share_count > 1 else 0
    block_range = jnp.arange(blocks_piece, dtype=jnp.int32)
    parts = [(weights_here, owner * blocks_here + jnp.arange(blocks_here, dtype=jnp.int32))]
    if share_count > 1:
        travelling = lax.dynamic_slice_in_dim(weights_here, group * piece, piece, axis=0)
    else:
        travelling = weights_here
    ring = [(source, (source + 1) % feat_count) for source in range(feat_count)]
    for step in range(1, feat_count):
        travelling = lax.ppermute(travelling, "feat", ring)
        source_block = (owner - step) % feat_count
        parts.append(
            (travelling, source_block * blocks_here + group * blocks_piece + block_range)
        )
        for shift in range(1, share_count):
            pairs = [(source, (source + shift) % group_count) for source in range(group_count)]
            forwarded = lax.ppermute(travelling, "groups", pairs)
            from_group = (group - shift) % group_count
            parts.append(
                (forwarded, source_block * blocks_here + from_group * blocks_piece + block_range)
            )
    return parts


def exchange_rows(first, second, feat_count):
    slots_here, row_count, _ = first.shape
    share = row_count // feat_count
    owner = lax.axis_index("feat")
    pieces, ids = [], []
    for shift in range(feat_count):
        target = (owner + shift) % feat_count
        piece = jnp.concatenate(
            [
                lax.dynamic_slice_in_dim(first, target * share, share, axis=1),
                lax.dynamic_slice_in_dim(second, target * share, share, axis=1),
            ],
            0,
        )
        if shift:
            piece = lax.ppermute(
                piece, "feat", [(source, (source + shift) % feat_count) for source in range(feat_count)]
            )
        source = (owner - shift) % feat_count
        local = jnp.arange(slots_here, dtype=jnp.int32)
        ids.append(
            jnp.concatenate([source * slots_here + local, (feat_count + source) * slots_here + local])
        )
        pieces.append(piece)
    return pieces, ids


def on_device(
    pooled_first,
    pooled_second,
    feature_order,
    cross_down,
    cross_up,
    cross_bias,
    compress_weight,
    compress_bias,
    dense_vector,
    mlp_weight,
    mlp_bias,
    *,
    feat_count,
    group_count,
    tower_count,
):
    entry_count = pooled_first.shape[3]
    rows_here = cross_down.shape[1]
    rank = cross_down.shape[2]
    split = rows_here % group_count == 0 and (rows_here // group_count) % entry_count == 0
    share_count = group_count if split else 1

    hidden_pieces = [mlp_weight]
    for shift in range(1, tower_count):
        pairs = [(source, (source + shift) % tower_count) for source in range(tower_count)]
        hidden_pieces.append(lax.ppermute(mlp_weight, "tower", pairs))

    weights_here = jnp.concatenate([cross_down[0], cross_up[0], compress_weight[0]], axis=1)
    parts = weight_parts(weights_here, feat_count, group_count, share_count, entry_count)

    last_rows = parts[-1][0]
    first_rows, second_rows, last_rows = lax.optimization_barrier(
        (pooled_first[0], pooled_second[0], last_rows)
    )
    parts[-1] = (last_rows, parts[-1][1])
    pieces, slot_ids = exchange_rows(first_rows, second_rows, feat_count)
    row_count = pieces[0].shape[1]
    slot_count = sum(piece.shape[0] for piece in pieces)
    bias_blocks = cross_bias[0].reshape(slot_count, entry_count)
    features = jnp.concatenate([part_features for _, part_features in parts])
    position_count = features.shape[0]

    if len(pieces) > 4:
        pieces, slot_ids = [jnp.concatenate(pieces, 0)], [jnp.concatenate(slot_ids)]
    base_sum = None
    for piece, ids in zip(pieces, slot_ids):
        orders = feature_order[0][ids]
        one_hot = (orders[None, :] == features[:, None]).astype(jnp.bfloat16)
        term = jnp.einsum("fs,sre->rfe", one_hot, piece, preferred_element_type=jnp.float32)
        base_sum = term if base_sum is None else base_sum + term
    base_all = base_sum.astype(jnp.bfloat16).reshape(row_count, position_count * entry_count)

    bases = []
    low_sum = None
    offset = 0
    for rows, part_features in parts:
        width = part_features.shape[0] * entry_count
        base = base_all[:, offset : offset + width]
        offset += width
        bases.append(base)
        term = jnp.dot(base, rows[:, :rank], preferred_element_type=jnp.float32)
        low_sum = term if low_sum is None else low_sum + term
    low_rank = low_sum.astype(jnp.bfloat16)

    squeezed = None
    for (rows, features), base in zip(parts, bases):
        lifted = lax.dot_general(
            low_rank,
            rows[:, rank : 2 * rank],
            (((1,), (1,)), ((), ())),
            preferred_element_type=jnp.float32,
        )
        shift_row = bias_blocks[features].reshape(features.shape[0] * entry_count)
        columns = base.astype(jnp.float32)
        crossed = (columns * (lifted + shift_row[None, :]) + columns).astype(jnp.bfloat16)
        term = jnp.dot(crossed, rows[:, 2 * rank :], preferred_element_type=jnp.float32)
        squeezed = term if squeezed is None else squeezed + term
    compressed = (squeezed + compress_bias[0][None, :]).astype(jnp.bfloat16)
    gathered = lax.all_to_all(compressed, "tower", split_axis=0, concat_axis=1, tiled=True)
    local_rows = gathered.shape[0]
    vector_count = gathered.shape[1] // entry_count
    vectors = gathered.reshape(local_rows, vector_count, entry_count)
    gram_matrix = jnp.einsum(
        "bie,bje->bij", vectors, vectors, preferred_element_type=jnp.float32
    ) * (1.0 / math.sqrt(entry_count))
    pair_terms = gram_matrix.reshape(local_rows, vector_count * vector_count)[
        :, pair_positions(vector_count)
    ]
    joined = jnp.concatenate([dense_vector.astype(jnp.float32), pair_terms], 1).astype(jnp.bfloat16)
    hidden_units = mlp_weight.shape[1]
    hidden_rows = mlp_weight.shape[0]
    tower = lax.axis_index("tower")
    hidden_sum = jnp.zeros((local_rows, hidden_units), jnp.float32)
    for shift, rows in enumerate(hidden_pieces):
        source = (tower - shift) % tower_count
        columns = lax.dynamic_slice_in_dim(joined, source * hidden_rows, hidden_rows, axis=1)
        hidden_sum = hidden_sum + jnp.dot(columns, rows, preferred_element_type=jnp.float32)
    return jax.nn.relu(hidden_sum + mlp_bias[None, :]).astype(jnp.bfloat16)


def solution(mesh):
    in_specs = (
        P("tower", "feat", "groups", None),
        P("tower", "feat", "groups", None),
        P("tower", None),
        P("tower", "feat", None),
        P("tower", "feat", None),
        P("tower", None),
        P("tower", "feat", None),
        P("tower", None),
        P(("groups", "feat", "tower"), None),
        P("tower", None),
        P(),
    )
    out_specs = P(("groups", "feat", "tower"), None)
    body = functools.partial(
        on_device, feat_count=mesh.shape["feat"],
        group_count=mesh.shape["groups"],
        tower_count=mesh.shape["tower"],
    )
    return jax.shard_map(body, mesh=mesh, in_specs=in_specs, out_specs=out_specs, check_vma=False)
```

```python
import functools
import math

import jax
import jax.numpy as jnp
import numpy as np
from jax import lax
from jax.sharding import PartitionSpec as P


def pair_positions(vector_count):
    upper_rows, upper_cols = np.triu_indices(vector_count, 1)
    return upper_rows * vector_count + upper_cols


def weight_parts(weights_here, feat_count, group_count, share_count, entry_count):
    rows_here = weights_here.shape[0]
    piece = rows_here // share_count
    blocks_here = rows_here // entry_count
    blocks_piece = piece // entry_count
    owner = lax.axis_index("feat")
    group = lax.axis_index("groups") if share_count > 1 else 0
    block_range = jnp.arange(blocks_piece, dtype=jnp.int32)
    parts = [(weights_here, owner * blocks_here + jnp.arange(blocks_here, dtype=jnp.int32))]
    if share_count > 1:
        travelling = lax.dynamic_slice_in_dim(weights_here, group * piece, piece, axis=0)
    else:
        travelling = weights_here
    ring = [(source, (source + 1) % feat_count) for source in range(feat_count)]
    for step in range(1, feat_count):
        travelling = lax.ppermute(travelling, "feat", ring)
        source_block = (owner - step) % feat_count
        parts.append(
            (travelling, source_block * blocks_here + group * blocks_piece + block_range)
        )
        for shift in range(1, share_count):
            pairs = [(source, (source + shift) % group_count) for source in range(group_count)]
            forwarded = lax.ppermute(travelling, "groups", pairs)
            from_group = (group - shift) % group_count
            parts.append(
                (forwarded, source_block * blocks_here + from_group * blocks_piece + block_range)
            )
    return parts, travelling


def exchange_rows(first, second, feat_count):
    slots_here, row_count, _ = first.shape
    share = row_count // feat_count
    owner = lax.axis_index("feat")
    pieces, ids = [], []
    for shift in range(feat_count):
        target = (owner + shift) % feat_count
        piece = jnp.concatenate(
            [
                lax.dynamic_slice_in_dim(first, target * share, share, axis=1),
                lax.dynamic_slice_in_dim(second, target * share, share, axis=1),
            ],
            0,
        )
        if shift:
            piece = lax.ppermute(
                piece, "feat", [(source, (source + shift) % feat_count) for source in range(feat_count)]
            )
        source = (owner - shift) % feat_count
        local = jnp.arange(slots_here, dtype=jnp.int32)
        ids.append(
            jnp.concatenate([source * slots_here + local, (feat_count + source) * slots_here + local])
        )
        pieces.append(piece)
    return pieces, ids


def on_device(
    pooled_first,
    pooled_second,
    feature_order,
    cross_down,
    cross_up,
    cross_bias,
    compress_weight,
    compress_bias,
    dense_vector,
    mlp_weight,
    mlp_bias,
    *,
    feat_count,
    group_count,
    tower_count,
):
    entry_count = pooled_first.shape[3]
    rows_here = cross_down.shape[1]
    rank = cross_down.shape[2]
    split = rows_here % group_count == 0 and (rows_here // group_count) % entry_count == 0
    share_count = group_count if split else 1

    hidden_pieces = [mlp_weight]
    for shift in range(1, tower_count):
        pairs = [(source, (source + shift) % tower_count) for source in range(tower_count)]
        hidden_pieces.append(lax.ppermute(mlp_weight, "tower", pairs))

    weights_here = jnp.concatenate([cross_down[0], cross_up[0], compress_weight[0]], axis=1)
    parts, last_rows = weight_parts(weights_here, feat_count, group_count, share_count, entry_count)

    first_rows, second_rows, _ = lax.optimization_barrier(
        (pooled_first[0], pooled_second[0], last_rows)
    )
    pieces, slot_ids = exchange_rows(first_rows, second_rows, feat_count)
    row_count = pieces[0].shape[1]
    slot_count = sum(piece.shape[0] for piece in pieces)
    bias_blocks = cross_bias[0].reshape(slot_count, entry_count)
    features = jnp.concatenate([part_features for _, part_features in parts])
    position_count = features.shape[0]

    if len(pieces) > 4:
        pieces, slot_ids = [jnp.concatenate(pieces, 0)], [jnp.concatenate(slot_ids)]
    base_sum = None
    for piece, ids in zip(pieces, slot_ids):
        orders = feature_order[0][ids]
        one_hot = (orders[None, :] == features[:, None]).astype(jnp.bfloat16)
        term = jnp.einsum("fs,sre->rfe", one_hot, piece, preferred_element_type=jnp.float32)
        base_sum = term if base_sum is None else base_sum + term
    base_all = base_sum.astype(jnp.bfloat16).reshape(row_count, position_count * entry_count)

    weights = jnp.concatenate([rows for rows, _ in parts], 0)
    low_sum = jnp.dot(base_all, weights[:, :rank], preferred_element_type=jnp.float32)
    low_rank = low_sum.astype(jnp.bfloat16)
    lifted = lax.dot_general(
        low_rank,
        weights[:, rank : 2 * rank],
        (((1,), (1,)), ((), ())),
        preferred_element_type=jnp.float32,
    )
    shift_row = bias_blocks[features].reshape(position_count * entry_count)
    columns = base_all.astype(jnp.float32)
    crossed = (columns * (lifted + shift_row[None, :]) + columns).astype(jnp.bfloat16)
    squeezed = jnp.dot(crossed, weights[:, 2 * rank :], preferred_element_type=jnp.float32)
    compressed = (squeezed + compress_bias[0][None, :]).astype(jnp.bfloat16)
    gathered = lax.all_to_all(compressed, "tower", split_axis=0, concat_axis=1, tiled=True)
    local_rows = gathered.shape[0]
    vector_count = gathered.shape[1] // entry_count
    vectors = gathered.reshape(local_rows, vector_count, entry_count)
    gram_matrix = jnp.einsum(
        "bie,bje->bij", vectors, vectors, preferred_element_type=jnp.float32
    ) * (1.0 / math.sqrt(entry_count))
    pair_terms = gram_matrix.reshape(local_rows, vector_count * vector_count)[
        :, pair_positions(vector_count)
    ]
    joined = jnp.concatenate([dense_vector.astype(jnp.float32), pair_terms], 1).astype(jnp.bfloat16)
    hidden_units = mlp_weight.shape[1]
    hidden_rows = mlp_weight.shape[0]
    tower = lax.axis_index("tower")
    hidden_sum = jnp.zeros((local_rows, hidden_units), jnp.float32)
    for shift, rows in enumerate(hidden_pieces):
        source = (tower - shift) % tower_count
        columns = lax.dynamic_slice_in_dim(joined, source * hidden_rows, hidden_rows, axis=1)
        hidden_sum = hidden_sum + jnp.dot(columns, rows, preferred_element_type=jnp.float32)
    return jax.nn.relu(hidden_sum + mlp_bias[None, :]).astype(jnp.bfloat16)


def solution(mesh):
    in_specs = (
        P("tower", "feat", "groups", None),
        P("tower", "feat", "groups", None),
        P("tower", None),
        P("tower", "feat", None),
        P("tower", "feat", None),
        P("tower", None),
        P("tower", "feat", None),
        P("tower", None),
        P(("groups", "feat", "tower"), None),
        P("tower", None),
        P(),
    )
    out_specs = P(("groups", "feat", "tower"), None)
    body = functools.partial(
        on_device, feat_count=mesh.shape["feat"],
        group_count=mesh.shape["groups"],
        tower_count=mesh.shape["tower"],
    )
    return jax.shard_map(body, mesh=mesh, in_specs=in_specs, out_specs=out_specs, check_vma=False)
```

```python
import functools
import math

import jax
import jax.numpy as jnp
import numpy as np
from jax import lax
from jax.sharding import PartitionSpec as P


def pair_positions(vector_count):
    upper_rows, upper_cols = np.triu_indices(vector_count, 1)
    return upper_rows * vector_count + upper_cols


def weight_parts(weights_here, feat_count, group_count, share_count, entry_count):
    rows_here = weights_here.shape[0]
    piece = rows_here // share_count
    blocks_here = rows_here // entry_count
    blocks_piece = piece // entry_count
    owner = lax.axis_index("feat")
    group = lax.axis_index("groups") if share_count > 1 else 0
    block_range = jnp.arange(blocks_piece, dtype=jnp.int32)
    parts = [(weights_here, owner * blocks_here + jnp.arange(blocks_here, dtype=jnp.int32))]
    if share_count > 1:
        travelling = lax.dynamic_slice_in_dim(weights_here, group * piece, piece, axis=0)
    else:
        travelling = weights_here
    ring = [(source, (source + 1) % feat_count) for source in range(feat_count)]
    released = travelling
    for step in range(1, feat_count):
        if step == feat_count - 1:
            released = travelling
        travelling = lax.ppermute(travelling, "feat", ring)
        source_block = (owner - step) % feat_count
        parts.append(
            (travelling, source_block * blocks_here + group * blocks_piece + block_range)
        )
        for shift in range(1, share_count):
            pairs = [(source, (source + shift) % group_count) for source in range(group_count)]
            forwarded = lax.ppermute(travelling, "groups", pairs)
            from_group = (group - shift) % group_count
            parts.append(
                (forwarded, source_block * blocks_here + from_group * blocks_piece + block_range)
            )
    return parts, released


def exchange_rows(first, second, feat_count):
    slots_here, row_count, _ = first.shape
    share = row_count // feat_count
    owner = lax.axis_index("feat")
    pieces, ids = [], []
    for shift in range(feat_count):
        target = (owner + shift) % feat_count
        piece = jnp.concatenate(
            [
                lax.dynamic_slice_in_dim(first, target * share, share, axis=1),
                lax.dynamic_slice_in_dim(second, target * share, share, axis=1),
            ],
            0,
        )
        if shift:
            piece = lax.ppermute(
                piece, "feat", [(source, (source + shift) % feat_count) for source in range(feat_count)]
            )
        source = (owner - shift) % feat_count
        local = jnp.arange(slots_here, dtype=jnp.int32)
        ids.append(
            jnp.concatenate([source * slots_here + local, (feat_count + source) * slots_here + local])
        )
        pieces.append(piece)
    return pieces, ids


def on_device(
    pooled_first,
    pooled_second,
    feature_order,
    cross_down,
    cross_up,
    cross_bias,
    compress_weight,
    compress_bias,
    dense_vector,
    mlp_weight,
    mlp_bias,
    *,
    feat_count,
    group_count,
    tower_count,
):
    entry_count = pooled_first.shape[3]
    rows_here = cross_down.shape[1]
    rank = cross_down.shape[2]
    split = rows_here % group_count == 0 and (rows_here // group_count) % entry_count == 0
    share_count = group_count if split else 1

    hidden_pieces = [mlp_weight]
    for shift in range(1, tower_count):
        pairs = [(source, (source + shift) % tower_count) for source in range(tower_count)]
        hidden_pieces.append(lax.ppermute(mlp_weight, "tower", pairs))

    weights_here = jnp.concatenate([cross_down[0], cross_up[0], compress_weight[0]], axis=1)
    parts, last_rows = weight_parts(weights_here, feat_count, group_count, share_count, entry_count)

    first_rows, second_rows, _ = lax.optimization_barrier(
        (pooled_first[0], pooled_second[0], last_rows)
    )
    pieces, slot_ids = exchange_rows(first_rows, second_rows, feat_count)
    row_count = pieces[0].shape[1]
    slot_count = sum(piece.shape[0] for piece in pieces)
    bias_blocks = cross_bias[0].reshape(slot_count, entry_count)
    features = jnp.concatenate([part_features for _, part_features in parts])
    position_count = features.shape[0]

    if len(pieces) > 4:
        pieces, slot_ids = [jnp.concatenate(pieces, 0)], [jnp.concatenate(slot_ids)]
    base_sum = None
    for piece, ids in zip(pieces, slot_ids):
        orders = feature_order[0][ids]
        one_hot = (orders[None, :] == features[:, None]).astype(jnp.bfloat16)
        term = jnp.einsum("fs,sre->rfe", one_hot, piece, preferred_element_type=jnp.float32)
        base_sum = term if base_sum is None else base_sum + term
    base_all = base_sum.astype(jnp.bfloat16).reshape(row_count, position_count * entry_count)

    weights = jnp.concatenate([rows for rows, _ in parts], 0)
    low_sum = jnp.dot(base_all, weights[:, :rank], preferred_element_type=jnp.float32)
    low_rank = low_sum.astype(jnp.bfloat16)
    lifted = lax.dot_general(
        low_rank,
        weights[:, rank : 2 * rank],
        (((1,), (1,)), ((), ())),
        preferred_element_type=jnp.float32,
    )
    shift_row = bias_blocks[features].reshape(position_count * entry_count)
    columns = base_all.astype(jnp.float32)
    crossed = (columns * (lifted + shift_row[None, :]) + columns).astype(jnp.bfloat16)
    squeezed = jnp.dot(crossed, weights[:, 2 * rank :], preferred_element_type=jnp.float32)
    compressed = (squeezed + compress_bias[0][None, :]).astype(jnp.bfloat16)
    gathered = lax.all_to_all(compressed, "tower", split_axis=0, concat_axis=1, tiled=True)
    local_rows = gathered.shape[0]
    vector_count = gathered.shape[1] // entry_count
    vectors = gathered.reshape(local_rows, vector_count, entry_count)
    gram_matrix = jnp.einsum(
        "bie,bje->bij", vectors, vectors, preferred_element_type=jnp.float32
    ) * (1.0 / math.sqrt(entry_count))
    pair_terms = gram_matrix.reshape(local_rows, vector_count * vector_count)[
        :, pair_positions(vector_count)
    ]
    joined = jnp.concatenate([dense_vector.astype(jnp.float32), pair_terms], 1).astype(jnp.bfloat16)
    hidden_units = mlp_weight.shape[1]
    hidden_rows = mlp_weight.shape[0]
    tower = lax.axis_index("tower")
    hidden_sum = jnp.zeros((local_rows, hidden_units), jnp.float32)
    for shift, rows in enumerate(hidden_pieces):
        source = (tower - shift) % tower_count
        columns = lax.dynamic_slice_in_dim(joined, source * hidden_rows, hidden_rows, axis=1)
        hidden_sum = hidden_sum + jnp.dot(columns, rows, preferred_element_type=jnp.float32)
    return jax.nn.relu(hidden_sum + mlp_bias[None, :]).astype(jnp.bfloat16)


def solution(mesh):
    in_specs = (
        P("tower", "feat", "groups", None),
        P("tower", "feat", "groups", None),
        P("tower", None),
        P("tower", "feat", None),
        P("tower", "feat", None),
        P("tower", None),
        P("tower", "feat", None),
        P("tower", None),
        P(("groups", "feat", "tower"), None),
        P("tower", None),
        P(),
    )
    out_specs = P(("groups", "feat", "tower"), None)
    body = functools.partial(
        on_device, feat_count=mesh.shape["feat"],
        group_count=mesh.shape["groups"],
        tower_count=mesh.shape["tower"],
    )
    return jax.shard_map(body, mesh=mesh, in_specs=in_specs, out_specs=out_specs, check_vma=False)
```

```python
import functools
import math

import jax
import jax.numpy as jnp
import numpy as np
from jax import lax
from jax.sharding import PartitionSpec as P


def pair_positions(vector_count):
    upper_rows, upper_cols = np.triu_indices(vector_count, 1)
    return upper_rows * vector_count + upper_cols


def weight_parts(weights_here, feat_count, group_count, share_count, entry_count):
    rows_here = weights_here.shape[0]
    piece = rows_here // share_count
    blocks_here = rows_here // entry_count
    blocks_piece = piece // entry_count
    owner = lax.axis_index("feat")
    group = lax.axis_index("groups") if share_count > 1 else 0
    block_range = jnp.arange(blocks_piece, dtype=jnp.int32)
    parts = [(weights_here, owner * blocks_here + jnp.arange(blocks_here, dtype=jnp.int32))]
    if share_count > 1:
        travelling = lax.dynamic_slice_in_dim(weights_here, group * piece, piece, axis=0)
    else:
        travelling = weights_here
    ring = [(source, (source + 1) % feat_count) for source in range(feat_count)]
    for step in range(1, feat_count):
        travelling = lax.ppermute(travelling, "feat", ring)
        source_block = (owner - step) % feat_count
        parts.append(
            (travelling, source_block * blocks_here + group * blocks_piece + block_range)
        )
        for shift in range(1, share_count):
            pairs = [(source, (source + shift) % group_count) for source in range(group_count)]
            forwarded = lax.ppermute(travelling, "groups", pairs)
            from_group = (group - shift) % group_count
            parts.append(
                (forwarded, source_block * blocks_here + from_group * blocks_piece + block_range)
            )
    return parts, travelling


def exchange_rows(first, second, feat_count, gate):
    slots_here, row_count, _ = first.shape
    share = row_count // feat_count
    owner = lax.axis_index("feat")
    pieces, ids = [], []
    for shift in range(feat_count):
        target = (owner + shift) % feat_count
        pieces.append(
            jnp.concatenate(
                [
                    lax.dynamic_slice_in_dim(first, target * share, share, axis=1),
                    lax.dynamic_slice_in_dim(second, target * share, share, axis=1),
                ],
                0,
            )
        )
    pieces, _ = lax.optimization_barrier((pieces, gate))
    for shift in range(feat_count):
        if shift:
            pieces[shift] = lax.ppermute(
                pieces[shift],
                "feat",
                [(source, (source + shift) % feat_count) for source in range(feat_count)],
            )
        source = (owner - shift) % feat_count
        local = jnp.arange(slots_here, dtype=jnp.int32)
        ids.append(
            jnp.concatenate([source * slots_here + local, (feat_count + source) * slots_here + local])
        )
    return pieces, ids


def on_device(
    pooled_first,
    pooled_second,
    feature_order,
    cross_down,
    cross_up,
    cross_bias,
    compress_weight,
    compress_bias,
    dense_vector,
    mlp_weight,
    mlp_bias,
    *,
    feat_count,
    group_count,
    tower_count,
):
    entry_count = pooled_first.shape[3]
    rows_here = cross_down.shape[1]
    rank = cross_down.shape[2]
    split = rows_here % group_count == 0 and (rows_here // group_count) % entry_count == 0
    share_count = group_count if split else 1

    hidden_pieces = [mlp_weight]
    for shift in range(1, tower_count):
        pairs = [(source, (source + shift) % tower_count) for source in range(tower_count)]
        hidden_pieces.append(lax.ppermute(mlp_weight, "tower", pairs))

    weights_here = jnp.concatenate([cross_down[0], cross_up[0], compress_weight[0]], axis=1)
    parts, last_rows = weight_parts(weights_here, feat_count, group_count, share_count, entry_count)

    pieces, slot_ids = exchange_rows(pooled_first[0], pooled_second[0], feat_count, last_rows)
    row_count = pieces[0].shape[1]
    slot_count = sum(piece.shape[0] for piece in pieces)
    bias_blocks = cross_bias[0].reshape(slot_count, entry_count)
    features = jnp.concatenate([part_features for _, part_features in parts])
    position_count = features.shape[0]

    if len(pieces) > 4:
        pieces, slot_ids = [jnp.concatenate(pieces, 0)], [jnp.concatenate(slot_ids)]
    base_sum = None
    for piece, ids in zip(pieces, slot_ids):
        orders = feature_order[0][ids]
        one_hot = (orders[None, :] == features[:, None]).astype(jnp.bfloat16)
        term = jnp.einsum("fs,sre->rfe", one_hot, piece, preferred_element_type=jnp.float32)
        base_sum = term if base_sum is None else base_sum + term
    base_all = base_sum.astype(jnp.bfloat16).reshape(row_count, position_count * entry_count)

    weights = jnp.concatenate([rows for rows, _ in parts], 0)
    low_sum = jnp.dot(base_all, weights[:, :rank], preferred_element_type=jnp.float32)
    low_rank = low_sum.astype(jnp.bfloat16)
    lifted = lax.dot_general(
        low_rank,
        weights[:, rank : 2 * rank],
        (((1,), (1,)), ((), ())),
        preferred_element_type=jnp.float32,
    )
    shift_row = bias_blocks[features].reshape(position_count * entry_count)
    columns = base_all.astype(jnp.float32)
    crossed = (columns * (lifted + shift_row[None, :]) + columns).astype(jnp.bfloat16)
    squeezed = jnp.dot(crossed, weights[:, 2 * rank :], preferred_element_type=jnp.float32)
    compressed = (squeezed + compress_bias[0][None, :]).astype(jnp.bfloat16)
    gathered = lax.all_to_all(compressed, "tower", split_axis=0, concat_axis=1, tiled=True)
    local_rows = gathered.shape[0]
    vector_count = gathered.shape[1] // entry_count
    vectors = gathered.reshape(local_rows, vector_count, entry_count)
    gram_matrix = jnp.einsum(
        "bie,bje->bij", vectors, vectors, preferred_element_type=jnp.float32
    ) * (1.0 / math.sqrt(entry_count))
    pair_terms = gram_matrix.reshape(local_rows, vector_count * vector_count)[
        :, pair_positions(vector_count)
    ]
    joined = jnp.concatenate([dense_vector.astype(jnp.float32), pair_terms], 1).astype(jnp.bfloat16)
    hidden_units = mlp_weight.shape[1]
    hidden_rows = mlp_weight.shape[0]
    tower = lax.axis_index("tower")
    hidden_sum = jnp.zeros((local_rows, hidden_units), jnp.float32)
    for shift, rows in enumerate(hidden_pieces):
        source = (tower - shift) % tower_count
        columns = lax.dynamic_slice_in_dim(joined, source * hidden_rows, hidden_rows, axis=1)
        hidden_sum = hidden_sum + jnp.dot(columns, rows, preferred_element_type=jnp.float32)
    return jax.nn.relu(hidden_sum + mlp_bias[None, :]).astype(jnp.bfloat16)


def solution(mesh):
    in_specs = (
        P("tower", "feat", "groups", None),
        P("tower", "feat", "groups", None),
        P("tower", None),
        P("tower", "feat", None),
        P("tower", "feat", None),
        P("tower", None),
        P("tower", "feat", None),
        P("tower", None),
        P(("groups", "feat", "tower"), None),
        P("tower", None),
        P(),
    )
    out_specs = P(("groups", "feat", "tower"), None)
    body = functools.partial(
        on_device, feat_count=mesh.shape["feat"],
        group_count=mesh.shape["groups"],
        tower_count=mesh.shape["tower"],
    )
    return jax.shard_map(body, mesh=mesh, in_specs=in_specs, out_specs=out_specs, check_vma=False)
```

```python
import functools
import math

import jax
import jax.numpy as jnp
import numpy as np
from jax import lax
from jax.sharding import PartitionSpec as P


def pair_positions(vector_count):
    upper_rows, upper_cols = np.triu_indices(vector_count, 1)
    return upper_rows * vector_count + upper_cols


def weight_parts(weights_here, feat_count, group_count, share_count, entry_count):
    rows_here = weights_here.shape[0]
    piece = rows_here // share_count
    blocks_here = rows_here // entry_count
    blocks_piece = piece // entry_count
    owner = lax.axis_index("feat")
    group = lax.axis_index("groups") if share_count > 1 else 0
    block_range = jnp.arange(blocks_piece, dtype=jnp.int32)
    parts = [(weights_here, owner * blocks_here + jnp.arange(blocks_here, dtype=jnp.int32))]
    if share_count > 1:
        travelling = lax.dynamic_slice_in_dim(weights_here, group * piece, piece, axis=0)
    else:
        travelling = weights_here
    chunk_count = 2 if blocks_piece % 2 == 0 else 1
    chunk_blocks = blocks_piece // chunk_count
    chunk_rows = chunk_blocks * entry_count
    chunk_range = jnp.arange(chunk_blocks, dtype=jnp.int32)
    rings = [
        lax.slice_in_dim(travelling, chunk * chunk_rows, (chunk + 1) * chunk_rows, axis=0)
        for chunk in range(chunk_count)
    ]
    ring = [(source, (source + 1) % feat_count) for source in range(feat_count)]
    for step in range(1, feat_count):
        source_block = (owner - step) % feat_count
        for chunk in range(chunk_count):
            rings[chunk] = lax.ppermute(rings[chunk], "feat", ring)
            first_block = source_block * blocks_here + chunk * chunk_blocks
            parts.append((rings[chunk], first_block + group * blocks_piece + chunk_range))
            for shift in range(1, share_count):
                pairs = [(source, (source + shift) % group_count) for source in range(group_count)]
                forwarded = lax.ppermute(rings[chunk], "groups", pairs)
                from_group = (group - shift) % group_count
                parts.append((forwarded, first_block + from_group * blocks_piece + chunk_range))
    travelling = rings
    return parts, travelling


def exchange_rows(first, second, feat_count):
    slots_here, row_count, _ = first.shape
    share = row_count // feat_count
    owner = lax.axis_index("feat")
    pieces, ids = [], []
    for shift in range(feat_count):
        target = (owner + shift) % feat_count
        piece = jnp.concatenate(
            [
                lax.dynamic_slice_in_dim(first, target * share, share, axis=1),
                lax.dynamic_slice_in_dim(second, target * share, share, axis=1),
            ],
            0,
        )
        if shift:
            piece = lax.ppermute(
                piece, "feat", [(source, (source + shift) % feat_count) for source in range(feat_count)]
            )
        source = (owner - shift) % feat_count
        local = jnp.arange(slots_here, dtype=jnp.int32)
        ids.append(
            jnp.concatenate([source * slots_here + local, (feat_count + source) * slots_here + local])
        )
        pieces.append(piece)
    return pieces, ids


def on_device(
    pooled_first,
    pooled_second,
    feature_order,
    cross_down,
    cross_up,
    cross_bias,
    compress_weight,
    compress_bias,
    dense_vector,
    mlp_weight,
    mlp_bias,
    *,
    feat_count,
    group_count,
    tower_count,
):
    entry_count = pooled_first.shape[3]
    rows_here = cross_down.shape[1]
    rank = cross_down.shape[2]
    split = rows_here % group_count == 0 and (rows_here // group_count) % entry_count == 0
    share_count = group_count if split else 1

    hidden_pieces = [mlp_weight]
    for shift in range(1, tower_count):
        pairs = [(source, (source + shift) % tower_count) for source in range(tower_count)]
        hidden_pieces.append(lax.ppermute(mlp_weight, "tower", pairs))

    weights_here = jnp.concatenate([cross_down[0], cross_up[0], compress_weight[0]], axis=1)
    parts, last_rows = weight_parts(weights_here, feat_count, group_count, share_count, entry_count)

    first_rows, second_rows, _ = lax.optimization_barrier(
        (pooled_first[0], pooled_second[0], last_rows)
    )
    pieces, slot_ids = exchange_rows(first_rows, second_rows, feat_count)
    row_count = pieces[0].shape[1]
    slot_count = sum(piece.shape[0] for piece in pieces)
    bias_blocks = cross_bias[0].reshape(slot_count, entry_count)
    features = jnp.concatenate([part_features for _, part_features in parts])
    position_count = features.shape[0]

    if len(pieces) > 4:
        pieces, slot_ids = [jnp.concatenate(pieces, 0)], [jnp.concatenate(slot_ids)]
    base_sum = None
    for piece, ids in zip(pieces, slot_ids):
        orders = feature_order[0][ids]
        one_hot = (orders[None, :] == features[:, None]).astype(jnp.bfloat16)
        term = jnp.einsum("fs,sre->rfe", one_hot, piece, preferred_element_type=jnp.float32)
        base_sum = term if base_sum is None else base_sum + term
    base_all = base_sum.astype(jnp.bfloat16).reshape(row_count, position_count * entry_count)

    weights = jnp.concatenate([rows for rows, _ in parts], 0)
    low_sum = jnp.dot(base_all, weights[:, :rank], preferred_element_type=jnp.float32)
    low_rank = low_sum.astype(jnp.bfloat16)
    lifted = lax.dot_general(
        low_rank,
        weights[:, rank : 2 * rank],
        (((1,), (1,)), ((), ())),
        preferred_element_type=jnp.float32,
    )
    shift_row = bias_blocks[features].reshape(position_count * entry_count)
    columns = base_all.astype(jnp.float32)
    crossed = (columns * (lifted + shift_row[None, :]) + columns).astype(jnp.bfloat16)
    squeezed = jnp.dot(crossed, weights[:, 2 * rank :], preferred_element_type=jnp.float32)
    compressed = (squeezed + compress_bias[0][None, :]).astype(jnp.bfloat16)
    gathered = lax.all_to_all(compressed, "tower", split_axis=0, concat_axis=1, tiled=True)
    local_rows = gathered.shape[0]
    vector_count = gathered.shape[1] // entry_count
    vectors = gathered.reshape(local_rows, vector_count, entry_count)
    gram_matrix = jnp.einsum(
        "bie,bje->bij", vectors, vectors, preferred_element_type=jnp.float32
    ) * (1.0 / math.sqrt(entry_count))
    pair_terms = gram_matrix.reshape(local_rows, vector_count * vector_count)[
        :, pair_positions(vector_count)
    ]
    joined = jnp.concatenate([dense_vector.astype(jnp.float32), pair_terms], 1).astype(jnp.bfloat16)
    hidden_units = mlp_weight.shape[1]
    hidden_rows = mlp_weight.shape[0]
    tower = lax.axis_index("tower")
    hidden_sum = jnp.zeros((local_rows, hidden_units), jnp.float32)
    for shift, rows in enumerate(hidden_pieces):
        source = (tower - shift) % tower_count
        columns = lax.dynamic_slice_in_dim(joined, source * hidden_rows, hidden_rows, axis=1)
        hidden_sum = hidden_sum + jnp.dot(columns, rows, preferred_element_type=jnp.float32)
    return jax.nn.relu(hidden_sum + mlp_bias[None, :]).astype(jnp.bfloat16)


def solution(mesh):
    in_specs = (
        P("tower", "feat", "groups", None),
        P("tower", "feat", "groups", None),
        P("tower", None),
        P("tower", "feat", None),
        P("tower", "feat", None),
        P("tower", None),
        P("tower", "feat", None),
        P("tower", None),
        P(("groups", "feat", "tower"), None),
        P("tower", None),
        P(),
    )
    out_specs = P(("groups", "feat", "tower"), None)
    body = functools.partial(
        on_device, feat_count=mesh.shape["feat"],
        group_count=mesh.shape["groups"],
        tower_count=mesh.shape["tower"],
    )
    return jax.shard_map(body, mesh=mesh, in_specs=in_specs, out_specs=out_specs, check_vma=False)
```

```python
import functools
import math

import jax
import jax.numpy as jnp
import numpy as np
from jax import lax
from jax.sharding import PartitionSpec as P


def pair_positions(vector_count):
    upper_rows, upper_cols = np.triu_indices(vector_count, 1)
    return upper_rows * vector_count + upper_cols


def weight_parts(weights_here, feat_count, group_count, share_count, entry_count):
    rows_here = weights_here.shape[0]
    piece = rows_here // share_count
    blocks_here = rows_here // entry_count
    blocks_piece = piece // entry_count
    owner = lax.axis_index("feat")
    group = lax.axis_index("groups") if share_count > 1 else 0
    block_range = jnp.arange(blocks_piece, dtype=jnp.int32)
    parts = [(weights_here, owner * blocks_here + jnp.arange(blocks_here, dtype=jnp.int32))]
    if share_count > 1:
        travelling = lax.dynamic_slice_in_dim(weights_here, group * piece, piece, axis=0)
    else:
        travelling = weights_here
    chunk_count = next(count for count in (4, 2, 1) if blocks_piece % count == 0)
    chunk_blocks = blocks_piece // chunk_count
    chunk_rows = chunk_blocks * entry_count
    chunk_range = jnp.arange(chunk_blocks, dtype=jnp.int32)
    rings = [
        lax.slice_in_dim(travelling, chunk * chunk_rows, (chunk + 1) * chunk_rows, axis=0)
        for chunk in range(chunk_count)
    ]
    ring = [(source, (source + 1) % feat_count) for source in range(feat_count)]
    for step in range(1, feat_count):
        source_block = (owner - step) % feat_count
        for chunk in range(chunk_count):
            rings[chunk] = lax.ppermute(rings[chunk], "feat", ring)
            first_block = source_block * blocks_here + chunk * chunk_blocks
            parts.append((rings[chunk], first_block + group * blocks_piece + chunk_range))
            for shift in range(1, share_count):
                pairs = [(source, (source + shift) % group_count) for source in range(group_count)]
                forwarded = lax.ppermute(rings[chunk], "groups", pairs)
                from_group = (group - shift) % group_count
                parts.append((forwarded, first_block + from_group * blocks_piece + chunk_range))
    travelling = rings
    return parts, travelling


def exchange_rows(first, second, feat_count):
    slots_here, row_count, _ = first.shape
    share = row_count // feat_count
    owner = lax.axis_index("feat")
    pieces, ids = [], []
    for shift in range(feat_count):
        target = (owner + shift) % feat_count
        piece = jnp.concatenate(
            [
                lax.dynamic_slice_in_dim(first, target * share, share, axis=1),
                lax.dynamic_slice_in_dim(second, target * share, share, axis=1),
            ],
            0,
        )
        if shift:
            piece = lax.ppermute(
                piece, "feat", [(source, (source + shift) % feat_count) for source in range(feat_count)]
            )
        source = (owner - shift) % feat_count
        local = jnp.arange(slots_here, dtype=jnp.int32)
        ids.append(
            jnp.concatenate([source * slots_here + local, (feat_count + source) * slots_here + local])
        )
        pieces.append(piece)
    return pieces, ids


def on_device(
    pooled_first,
    pooled_second,
    feature_order,
    cross_down,
    cross_up,
    cross_bias,
    compress_weight,
    compress_bias,
    dense_vector,
    mlp_weight,
    mlp_bias,
    *,
    feat_count,
    group_count,
    tower_count,
):
    entry_count = pooled_first.shape[3]
    rows_here = cross_down.shape[1]
    rank = cross_down.shape[2]
    split = rows_here % group_count == 0 and (rows_here // group_count) % entry_count == 0
    share_count = group_count if split else 1

    hidden_pieces = [mlp_weight]
    for shift in range(1, tower_count):
        pairs = [(source, (source + shift) % tower_count) for source in range(tower_count)]
        hidden_pieces.append(lax.ppermute(mlp_weight, "tower", pairs))

    weights_here = jnp.concatenate([cross_down[0], cross_up[0], compress_weight[0]], axis=1)
    parts, last_rows = weight_parts(weights_here, feat_count, group_count, share_count, entry_count)

    first_rows, second_rows, _ = lax.optimization_barrier(
        (pooled_first[0], pooled_second[0], last_rows)
    )
    pieces, slot_ids = exchange_rows(first_rows, second_rows, feat_count)
    row_count = pieces[0].shape[1]
    slot_count = sum(piece.shape[0] for piece in pieces)
    bias_blocks = cross_bias[0].reshape(slot_count, entry_count)
    features = jnp.concatenate([part_features for _, part_features in parts])
    position_count = features.shape[0]

    if len(pieces) > 4:
        pieces, slot_ids = [jnp.concatenate(pieces, 0)], [jnp.concatenate(slot_ids)]
    base_sum = None
    for piece, ids in zip(pieces, slot_ids):
        orders = feature_order[0][ids]
        one_hot = (orders[None, :] == features[:, None]).astype(jnp.bfloat16)
        term = jnp.einsum("fs,sre->rfe", one_hot, piece, preferred_element_type=jnp.float32)
        base_sum = term if base_sum is None else base_sum + term
    base_all = base_sum.astype(jnp.bfloat16).reshape(row_count, position_count * entry_count)

    weights = jnp.concatenate([rows for rows, _ in parts], 0)
    low_sum = jnp.dot(base_all, weights[:, :rank], preferred_element_type=jnp.float32)
    low_rank = low_sum.astype(jnp.bfloat16)
    lifted = lax.dot_general(
        low_rank,
        weights[:, rank : 2 * rank],
        (((1,), (1,)), ((), ())),
        preferred_element_type=jnp.float32,
    )
    shift_row = bias_blocks[features].reshape(position_count * entry_count)
    columns = base_all.astype(jnp.float32)
    crossed = (columns * (lifted + shift_row[None, :]) + columns).astype(jnp.bfloat16)
    squeezed = jnp.dot(crossed, weights[:, 2 * rank :], preferred_element_type=jnp.float32)
    compressed = (squeezed + compress_bias[0][None, :]).astype(jnp.bfloat16)
    gathered = lax.all_to_all(compressed, "tower", split_axis=0, concat_axis=1, tiled=True)
    local_rows = gathered.shape[0]
    vector_count = gathered.shape[1] // entry_count
    vectors = gathered.reshape(local_rows, vector_count, entry_count)
    gram_matrix = jnp.einsum(
        "bie,bje->bij", vectors, vectors, preferred_element_type=jnp.float32
    ) * (1.0 / math.sqrt(entry_count))
    pair_terms = gram_matrix.reshape(local_rows, vector_count * vector_count)[
        :, pair_positions(vector_count)
    ]
    joined = jnp.concatenate([dense_vector.astype(jnp.float32), pair_terms], 1).astype(jnp.bfloat16)
    hidden_units = mlp_weight.shape[1]
    hidden_rows = mlp_weight.shape[0]
    tower = lax.axis_index("tower")
    hidden_sum = jnp.zeros((local_rows, hidden_units), jnp.float32)
    for shift, rows in enumerate(hidden_pieces):
        source = (tower - shift) % tower_count
        columns = lax.dynamic_slice_in_dim(joined, source * hidden_rows, hidden_rows, axis=1)
        hidden_sum = hidden_sum + jnp.dot(columns, rows, preferred_element_type=jnp.float32)
    return jax.nn.relu(hidden_sum + mlp_bias[None, :]).astype(jnp.bfloat16)


def solution(mesh):
    in_specs = (
        P("tower", "feat", "groups", None),
        P("tower", "feat", "groups", None),
        P("tower", None),
        P("tower", "feat", None),
        P("tower", "feat", None),
        P("tower", None),
        P("tower", "feat", None),
        P("tower", None),
        P(("groups", "feat", "tower"), None),
        P("tower", None),
        P(),
    )
    out_specs = P(("groups", "feat", "tower"), None)
    body = functools.partial(
        on_device, feat_count=mesh.shape["feat"],
        group_count=mesh.shape["groups"],
        tower_count=mesh.shape["tower"],
    )
    return jax.shard_map(body, mesh=mesh, in_specs=in_specs, out_specs=out_specs, check_vma=False)
```

```python
import functools
import math

import jax
import jax.numpy as jnp
import numpy as np
from jax import lax
from jax.sharding import PartitionSpec as P


def pair_positions(vector_count):
    upper_rows, upper_cols = np.triu_indices(vector_count, 1)
    return upper_rows * vector_count + upper_cols


def weight_parts(weights_here, feat_count, group_count, share_count, entry_count):
    rows_here = weights_here.shape[0]
    piece = rows_here // share_count
    blocks_here = rows_here // entry_count
    blocks_piece = piece // entry_count
    owner = lax.axis_index("feat")
    group = lax.axis_index("groups") if share_count > 1 else 0
    block_range = jnp.arange(blocks_piece, dtype=jnp.int32)
    parts = [(weights_here, owner * blocks_here + jnp.arange(blocks_here, dtype=jnp.int32))]
    if share_count > 1:
        travelling = lax.dynamic_slice_in_dim(weights_here, group * piece, piece, axis=0)
    else:
        travelling = weights_here
    chunk_count = next(count for count in (4, 2, 1) if blocks_piece % count == 0)
    chunk_blocks = blocks_piece // chunk_count
    chunk_rows = chunk_blocks * entry_count
    chunk_range = jnp.arange(chunk_blocks, dtype=jnp.int32)
    rings = [
        lax.slice_in_dim(travelling, chunk * chunk_rows, (chunk + 1) * chunk_rows, axis=0)
        for chunk in range(chunk_count)
    ]
    ring = [(source, (source + 1) % feat_count) for source in range(feat_count)]
    for step in range(1, feat_count):
        source_block = (owner - step) % feat_count
        for chunk in range(chunk_count):
            rings[chunk] = lax.ppermute(rings[chunk], "feat", ring)
            first_block = source_block * blocks_here + chunk * chunk_blocks
            parts.append((rings[chunk], first_block + group * blocks_piece + chunk_range))
            for shift in range(1, share_count):
                pairs = [(source, (source + shift) % group_count) for source in range(group_count)]
                forwarded = lax.ppermute(rings[chunk], "groups", pairs)
                from_group = (group - shift) % group_count
                parts.append((forwarded, first_block + from_group * blocks_piece + chunk_range))
    travelling = rings
    return parts, travelling


def exchange_rows(first, second, feat_count, tower_count, half, half_count, gate):
    slots_here, row_count, _ = first.shape
    share = row_count // feat_count
    owner = lax.axis_index("feat")
    pieces, ids = [], []
    for shift in range(feat_count):
        target = (owner + shift) % feat_count
        piece = jnp.concatenate(
            [
                lax.dynamic_slice_in_dim(first, target * share, share, axis=1),
                lax.dynamic_slice_in_dim(second, target * share, share, axis=1),
            ],
            0,
        )
        block = share // (tower_count * half_count)
        piece = piece.reshape(piece.shape[0], tower_count, half_count, block, piece.shape[2])
        piece = piece[:, :, half].reshape(piece.shape[0], tower_count * block, piece.shape[4])
        pieces.append(piece)
    pieces, _ = lax.optimization_barrier((pieces, gate))
    for shift in range(feat_count):
        piece = pieces[shift]
        if shift:
            piece = lax.ppermute(
                piece, "feat", [(source, (source + shift) % feat_count) for source in range(feat_count)]
            )
        source = (owner - shift) % feat_count
        local = jnp.arange(slots_here, dtype=jnp.int32)
        ids.append(
            jnp.concatenate([source * slots_here + local, (feat_count + source) * slots_here + local])
        )
        pieces[shift] = piece
    return pieces, ids


def on_device(
    pooled_first,
    pooled_second,
    feature_order,
    cross_down,
    cross_up,
    cross_bias,
    compress_weight,
    compress_bias,
    dense_vector,
    mlp_weight,
    mlp_bias,
    *,
    feat_count,
    group_count,
    tower_count,
):
    entry_count = pooled_first.shape[3]
    rows_here = cross_down.shape[1]
    rank = cross_down.shape[2]
    split = rows_here % group_count == 0 and (rows_here // group_count) % entry_count == 0
    share_count = group_count if split else 1

    hidden_pieces = [mlp_weight]
    for shift in range(1, tower_count):
        pairs = [(source, (source + shift) % tower_count) for source in range(tower_count)]
        hidden_pieces.append(lax.ppermute(mlp_weight, "tower", pairs))

    weights_here = jnp.concatenate([cross_down[0], cross_up[0], compress_weight[0]], axis=1)
    parts, last_rows = weight_parts(weights_here, feat_count, group_count, share_count, entry_count)

    features = jnp.concatenate([part_features for _, part_features in parts])
    position_count = features.shape[0]
    width = cross_bias.shape[1]
    bias_blocks = cross_bias[0].reshape(width // entry_count, entry_count)
    shift_row = bias_blocks[features].reshape(position_count * entry_count)
    weights = jnp.concatenate([rows for rows, _ in parts], 0)
    share = pooled_first.shape[2] // feat_count
    half_count = 2 if share % (2 * tower_count) == 0 else 1
    local_block = dense_vector.shape[0] // half_count
    hidden_units = mlp_weight.shape[1]
    hidden_rows = mlp_weight.shape[0]
    tower = lax.axis_index("tower")

    gate = last_rows
    outputs = []
    for half in range(half_count):
        pieces, slot_ids = exchange_rows(
            pooled_first[0], pooled_second[0], feat_count, tower_count, half, half_count, gate
        )
        gate = pieces
        row_count = pieces[0].shape[1]
        if len(pieces) > 4:
            pieces, slot_ids = [jnp.concatenate(pieces, 0)], [jnp.concatenate(slot_ids)]
        base_sum = None
        for piece, ids in zip(pieces, slot_ids):
            orders = feature_order[0][ids]
            one_hot = (orders[None, :] == features[:, None]).astype(jnp.bfloat16)
            term = jnp.einsum("fs,sre->rfe", one_hot, piece, preferred_element_type=jnp.float32)
            base_sum = term if base_sum is None else base_sum + term
        base_all = base_sum.astype(jnp.bfloat16).reshape(row_count, position_count * entry_count)

        low_sum = jnp.dot(base_all, weights[:, :rank], preferred_element_type=jnp.float32)
        low_rank = low_sum.astype(jnp.bfloat16)
        lifted = lax.dot_general(
            low_rank,
            weights[:, rank : 2 * rank],
            (((1,), (1,)), ((), ())),
            preferred_element_type=jnp.float32,
        )
        columns = base_all.astype(jnp.float32)
        crossed = (columns * (lifted + shift_row[None, :]) + columns).astype(jnp.bfloat16)
        squeezed = jnp.dot(crossed, weights[:, 2 * rank :], preferred_element_type=jnp.float32)
        compressed = (squeezed + compress_bias[0][None, :]).astype(jnp.bfloat16)
        gathered = lax.all_to_all(compressed, "tower", split_axis=0, concat_axis=1, tiled=True)
        local_rows = gathered.shape[0]
        vector_count = gathered.shape[1] // entry_count
        vectors = gathered.reshape(local_rows, vector_count, entry_count)
        gram_matrix = jnp.einsum(
            "bie,bje->bij", vectors, vectors, preferred_element_type=jnp.float32
        ) * (1.0 / math.sqrt(entry_count))
        pair_terms = gram_matrix.reshape(local_rows, vector_count * vector_count)[
            :, pair_positions(vector_count)
        ]
        dense_rows = lax.slice_in_dim(dense_vector, half * local_block, (half + 1) * local_block)
        joined = jnp.concatenate([dense_rows.astype(jnp.float32), pair_terms], 1).astype(
            jnp.bfloat16
        )
        hidden_sum = jnp.zeros((local_rows, hidden_units), jnp.float32)
        for shift, rows in enumerate(hidden_pieces):
            source = (tower - shift) % tower_count
            columns = lax.dynamic_slice_in_dim(joined, source * hidden_rows, hidden_rows, axis=1)
            hidden_sum = hidden_sum + jnp.dot(columns, rows, preferred_element_type=jnp.float32)
        outputs.append(jax.nn.relu(hidden_sum + mlp_bias[None, :]).astype(jnp.bfloat16))
    return jnp.concatenate(outputs, 0)


def solution(mesh):
    in_specs = (
        P("tower", "feat", "groups", None),
        P("tower", "feat", "groups", None),
        P("tower", None),
        P("tower", "feat", None),
        P("tower", "feat", None),
        P("tower", None),
        P("tower", "feat", None),
        P("tower", None),
        P(("groups", "feat", "tower"), None),
        P("tower", None),
        P(),
    )
    out_specs = P(("groups", "feat", "tower"), None)
    body = functools.partial(
        on_device, feat_count=mesh.shape["feat"],
        group_count=mesh.shape["groups"],
        tower_count=mesh.shape["tower"],
    )
    return jax.shard_map(body, mesh=mesh, in_specs=in_specs, out_specs=out_specs, check_vma=False)
```

```python
import functools
import math

import jax
import jax.numpy as jnp
import numpy as np
from jax import lax
from jax.sharding import PartitionSpec as P


def pair_positions(vector_count):
    upper_rows, upper_cols = np.triu_indices(vector_count, 1)
    return upper_rows * vector_count + upper_cols


def weight_parts(weights_here, feat_count, group_count, share_count, entry_count):
    rows_here = weights_here.shape[0]
    piece = rows_here // share_count
    blocks_here = rows_here // entry_count
    blocks_piece = piece // entry_count
    owner = lax.axis_index("feat")
    group = lax.axis_index("groups") if share_count > 1 else 0
    block_range = jnp.arange(blocks_piece, dtype=jnp.int32)
    parts = [(weights_here, owner * blocks_here + jnp.arange(blocks_here, dtype=jnp.int32))]
    if share_count > 1:
        travelling = lax.dynamic_slice_in_dim(weights_here, group * piece, piece, axis=0)
    else:
        travelling = weights_here
    chunk_count = next(count for count in (4, 2, 1) if blocks_piece % count == 0)
    chunk_blocks = blocks_piece // chunk_count
    chunk_rows = chunk_blocks * entry_count
    chunk_range = jnp.arange(chunk_blocks, dtype=jnp.int32)
    rings = [
        lax.slice_in_dim(travelling, chunk * chunk_rows, (chunk + 1) * chunk_rows, axis=0)
        for chunk in range(chunk_count)
    ]
    ring = [(source, (source + 1) % feat_count) for source in range(feat_count)]
    for step in range(1, feat_count):
        source_block = (owner - step) % feat_count
        for chunk in range(chunk_count):
            rings[chunk] = lax.ppermute(rings[chunk], "feat", ring)
            first_block = source_block * blocks_here + chunk * chunk_blocks
            parts.append((rings[chunk], first_block + group * blocks_piece + chunk_range))
            for shift in range(1, share_count):
                pairs = [(source, (source + shift) % group_count) for source in range(group_count)]
                forwarded = lax.ppermute(rings[chunk], "groups", pairs)
                from_group = (group - shift) % group_count
                parts.append((forwarded, first_block + from_group * blocks_piece + chunk_range))
    travelling = rings
    return parts, travelling


def exchange_rows(first, second, feat_count, tower_count, half, half_count, gate):
    slots_here, row_count, _ = first.shape
    share = row_count // feat_count
    owner = lax.axis_index("feat")
    pieces, ids = [], []
    for shift in range(feat_count):
        target = (owner + shift) % feat_count
        piece = jnp.concatenate(
            [
                lax.dynamic_slice_in_dim(first, target * share, share, axis=1),
                lax.dynamic_slice_in_dim(second, target * share, share, axis=1),
            ],
            0,
        )
        block = share // (tower_count * half_count)
        piece = piece.reshape(piece.shape[0], tower_count, half_count, block, piece.shape[2])
        piece = piece[:, :, half].reshape(piece.shape[0], tower_count * block, piece.shape[4])
        pieces.append(piece)
    pieces, _ = lax.optimization_barrier((pieces, gate))
    for shift in range(feat_count):
        piece = pieces[shift]
        if shift:
            piece = lax.ppermute(
                piece, "feat", [(source, (source + shift) % feat_count) for source in range(feat_count)]
            )
        source = (owner - shift) % feat_count
        local = jnp.arange(slots_here, dtype=jnp.int32)
        ids.append(
            jnp.concatenate([source * slots_here + local, (feat_count + source) * slots_here + local])
        )
        pieces[shift] = piece
    return pieces, ids


def on_device(
    pooled_first,
    pooled_second,
    feature_order,
    cross_down,
    cross_up,
    cross_bias,
    compress_weight,
    compress_bias,
    dense_vector,
    mlp_weight,
    mlp_bias,
    *,
    feat_count,
    group_count,
    tower_count,
):
    entry_count = pooled_first.shape[3]
    rows_here = cross_down.shape[1]
    rank = cross_down.shape[2]
    split = rows_here % group_count == 0 and (rows_here // group_count) % entry_count == 0
    share_count = group_count if split else 1

    hidden_pieces = [mlp_weight]
    for shift in range(1, tower_count):
        pairs = [(source, (source + shift) % tower_count) for source in range(tower_count)]
        hidden_pieces.append(lax.ppermute(mlp_weight, "tower", pairs))

    weights_here = jnp.concatenate([cross_down[0], cross_up[0], compress_weight[0]], axis=1)
    parts, last_rows = weight_parts(weights_here, feat_count, group_count, share_count, entry_count)

    features = jnp.concatenate([part_features for _, part_features in parts])
    position_count = features.shape[0]
    width = cross_bias.shape[1]
    bias_blocks = cross_bias[0].reshape(width // entry_count, entry_count)
    shift_row = bias_blocks[features].reshape(position_count * entry_count)
    weights = jnp.concatenate([rows for rows, _ in parts], 0)
    share = pooled_first.shape[2] // feat_count
    half_count = 2 if share % (2 * tower_count) == 0 else 1
    local_block = dense_vector.shape[0] // half_count
    hidden_units = mlp_weight.shape[1]
    hidden_rows = mlp_weight.shape[0]
    tower = lax.axis_index("tower")

    gate = (last_rows, hidden_pieces)
    outputs = []
    for half in range(half_count):
        pieces, slot_ids = exchange_rows(
            pooled_first[0], pooled_second[0], feat_count, tower_count, half, half_count, gate
        )
        gate = pieces
        row_count = pieces[0].shape[1]
        if len(pieces) > 4:
            pieces, slot_ids = [jnp.concatenate(pieces, 0)], [jnp.concatenate(slot_ids)]
        base_sum = None
        for piece, ids in zip(pieces, slot_ids):
            orders = feature_order[0][ids]
            one_hot = (orders[None, :] == features[:, None]).astype(jnp.bfloat16)
            term = jnp.einsum("fs,sre->rfe", one_hot, piece, preferred_element_type=jnp.float32)
            base_sum = term if base_sum is None else base_sum + term
        base_all = base_sum.astype(jnp.bfloat16).reshape(row_count, position_count * entry_count)

        low_sum = jnp.dot(base_all, weights[:, :rank], preferred_element_type=jnp.float32)
        low_rank = low_sum.astype(jnp.bfloat16)
        lifted = lax.dot_general(
            low_rank,
            weights[:, rank : 2 * rank],
            (((1,), (1,)), ((), ())),
            preferred_element_type=jnp.float32,
        )
        columns = base_all.astype(jnp.float32)
        crossed = (columns * (lifted + shift_row[None, :]) + columns).astype(jnp.bfloat16)
        squeezed = jnp.dot(crossed, weights[:, 2 * rank :], preferred_element_type=jnp.float32)
        compressed = (squeezed + compress_bias[0][None, :]).astype(jnp.bfloat16)
        gathered = lax.all_to_all(compressed, "tower", split_axis=0, concat_axis=1, tiled=True)
        local_rows = gathered.shape[0]
        vector_count = gathered.shape[1] // entry_count
        vectors = gathered.reshape(local_rows, vector_count, entry_count)
        gram_matrix = jnp.einsum(
            "bie,bje->bij", vectors, vectors, preferred_element_type=jnp.float32
        ) * (1.0 / math.sqrt(entry_count))
        pair_terms = gram_matrix.reshape(local_rows, vector_count * vector_count)[
            :, pair_positions(vector_count)
        ]
        dense_rows = lax.slice_in_dim(dense_vector, half * local_block, (half + 1) * local_block)
        joined = jnp.concatenate([dense_rows.astype(jnp.float32), pair_terms], 1).astype(
            jnp.bfloat16
        )
        hidden_sum = jnp.zeros((local_rows, hidden_units), jnp.float32)
        for shift, rows in enumerate(hidden_pieces):
            source = (tower - shift) % tower_count
            columns = lax.dynamic_slice_in_dim(joined, source * hidden_rows, hidden_rows, axis=1)
            hidden_sum = hidden_sum + jnp.dot(columns, rows, preferred_element_type=jnp.float32)
        outputs.append(jax.nn.relu(hidden_sum + mlp_bias[None, :]).astype(jnp.bfloat16))
    return jnp.concatenate(outputs, 0)


def solution(mesh):
    in_specs = (
        P("tower", "feat", "groups", None),
        P("tower", "feat", "groups", None),
        P("tower", None),
        P("tower", "feat", None),
        P("tower", "feat", None),
        P("tower", None),
        P("tower", "feat", None),
        P("tower", None),
        P(("groups", "feat", "tower"), None),
        P("tower", None),
        P(),
    )
    out_specs = P(("groups", "feat", "tower"), None)
    body = functools.partial(
        on_device, feat_count=mesh.shape["feat"],
        group_count=mesh.shape["groups"],
        tower_count=mesh.shape["tower"],
    )
    return jax.shard_map(body, mesh=mesh, in_specs=in_specs, out_specs=out_specs, check_vma=False)
```

```python
import functools
import math

import jax
import jax.numpy as jnp
import numpy as np
from jax import lax
from jax.sharding import PartitionSpec as P


def pair_positions(vector_count):
    upper_rows, upper_cols = np.triu_indices(vector_count, 1)
    return upper_rows * vector_count + upper_cols


def weight_parts(weight_list, feat_count, group_count, share_count, entry_count):
    rows_here = weight_list[0].shape[0]
    piece = rows_here // share_count
    blocks_here = rows_here // entry_count
    blocks_piece = piece // entry_count
    owner = lax.axis_index("feat")
    group = lax.axis_index("groups") if share_count > 1 else 0
    block_range = jnp.arange(blocks_piece, dtype=jnp.int32)
    chunk_count = next(count for count in (4, 2, 1) if blocks_piece % count == 0)
    chunk_blocks = blocks_piece // chunk_count
    chunk_rows = chunk_blocks * entry_count
    chunk_range = jnp.arange(chunk_blocks, dtype=jnp.int32)
    rings = [
        jnp.concatenate(
            [
                lax.dynamic_slice_in_dim(
                    weight, group * piece + chunk * chunk_rows, chunk_rows, axis=0
                )
                for weight in weight_list
            ],
            axis=1,
        )
        for chunk in range(chunk_count)
    ]
    weights_here = jnp.concatenate(weight_list, axis=1)
    parts = [(weights_here, owner * blocks_here + jnp.arange(blocks_here, dtype=jnp.int32))]
    ring = [(source, (source + 1) % feat_count) for source in range(feat_count)]
    for step in range(1, feat_count):
        source_block = (owner - step) % feat_count
        for chunk in range(chunk_count):
            rings[chunk] = lax.ppermute(rings[chunk], "feat", ring)
            first_block = source_block * blocks_here + chunk * chunk_blocks
            parts.append((rings[chunk], first_block + group * blocks_piece + chunk_range))
            for shift in range(1, share_count):
                pairs = [(source, (source + shift) % group_count) for source in range(group_count)]
                forwarded = lax.ppermute(rings[chunk], "groups", pairs)
                from_group = (group - shift) % group_count
                parts.append((forwarded, first_block + from_group * blocks_piece + chunk_range))
    travelling = rings
    return parts, travelling


def exchange_rows(first, second, feat_count):
    slots_here, row_count, _ = first.shape
    share = row_count // feat_count
    owner = lax.axis_index("feat")
    pieces, ids = [], []
    for shift in range(feat_count):
        target = (owner + shift) % feat_count
        piece = jnp.concatenate(
            [
                lax.dynamic_slice_in_dim(first, target * share, share, axis=1),
                lax.dynamic_slice_in_dim(second, target * share, share, axis=1),
            ],
            0,
        )
        if shift:
            piece = lax.ppermute(
                piece, "feat", [(source, (source + shift) % feat_count) for source in range(feat_count)]
            )
        source = (owner - shift) % feat_count
        local = jnp.arange(slots_here, dtype=jnp.int32)
        ids.append(
            jnp.concatenate([source * slots_here + local, (feat_count + source) * slots_here + local])
        )
        pieces.append(piece)
    return pieces, ids


def on_device(
    pooled_first,
    pooled_second,
    feature_order,
    cross_down,
    cross_up,
    cross_bias,
    compress_weight,
    compress_bias,
    dense_vector,
    mlp_weight,
    mlp_bias,
    *,
    feat_count,
    group_count,
    tower_count,
):
    entry_count = pooled_first.shape[3]
    rows_here = cross_down.shape[1]
    rank = cross_down.shape[2]
    split = rows_here % group_count == 0 and (rows_here // group_count) % entry_count == 0
    share_count = group_count if split else 1

    hidden_pieces = [mlp_weight]
    for shift in range(1, tower_count):
        pairs = [(source, (source + shift) % tower_count) for source in range(tower_count)]
        hidden_pieces.append(lax.ppermute(mlp_weight, "tower", pairs))

    weight_list = [cross_down[0], cross_up[0], compress_weight[0]]
    parts, last_rows = weight_parts(weight_list, feat_count, group_count, share_count, entry_count)

    first_rows, second_rows, _ = lax.optimization_barrier(
        (pooled_first[0], pooled_second[0], (last_rows, hidden_pieces))
    )
    pieces, slot_ids = exchange_rows(first_rows, second_rows, feat_count)
    row_count = pieces[0].shape[1]
    slot_count = sum(piece.shape[0] for piece in pieces)
    bias_blocks = cross_bias[0].reshape(slot_count, entry_count)
    features = jnp.concatenate([part_features for _, part_features in parts])
    position_count = features.shape[0]

    if len(pieces) > 4:
        pieces, slot_ids = [jnp.concatenate(pieces, 0)], [jnp.concatenate(slot_ids)]
    base_sum = None
    for piece, ids in zip(pieces, slot_ids):
        orders = feature_order[0][ids]
        one_hot = (orders[None, :] == features[:, None]).astype(jnp.bfloat16)
        term = jnp.einsum("fs,sre->rfe", one_hot, piece, preferred_element_type=jnp.float32)
        base_sum = term if base_sum is None else base_sum + term
    base_all = base_sum.astype(jnp.bfloat16).reshape(row_count, position_count * entry_count)

    weights = jnp.concatenate([rows for rows, _ in parts], 0)
    low_sum = jnp.dot(base_all, weights[:, :rank], preferred_element_type=jnp.float32)
    low_rank = low_sum.astype(jnp.bfloat16)
    lifted = lax.dot_general(
        low_rank,
        weights[:, rank : 2 * rank],
        (((1,), (1,)), ((), ())),
        preferred_element_type=jnp.float32,
    )
    shift_row = bias_blocks[features].reshape(position_count * entry_count)
    columns = base_all.astype(jnp.float32)
    crossed = (columns * (lifted + shift_row[None, :]) + columns).astype(jnp.bfloat16)
    squeezed = jnp.dot(crossed, weights[:, 2 * rank :], preferred_element_type=jnp.float32)
    compressed = (squeezed + compress_bias[0][None, :]).astype(jnp.bfloat16)
    gathered = lax.all_to_all(compressed, "tower", split_axis=0, concat_axis=1, tiled=True)
    local_rows = gathered.shape[0]
    vector_count = gathered.shape[1] // entry_count
    vectors = gathered.reshape(local_rows, vector_count, entry_count)
    gram_matrix = jnp.einsum(
        "bie,bje->bij", vectors, vectors, preferred_element_type=jnp.float32
    ) * (1.0 / math.sqrt(entry_count))
    pair_terms = gram_matrix.reshape(local_rows, vector_count * vector_count)[
        :, pair_positions(vector_count)
    ]
    joined = jnp.concatenate([dense_vector.astype(jnp.float32), pair_terms], 1).astype(jnp.bfloat16)
    hidden_units = mlp_weight.shape[1]
    hidden_rows = mlp_weight.shape[0]
    tower = lax.axis_index("tower")
    hidden_sum = jnp.zeros((local_rows, hidden_units), jnp.float32)
    for shift, rows in enumerate(hidden_pieces):
        source = (tower - shift) % tower_count
        columns = lax.dynamic_slice_in_dim(joined, source * hidden_rows, hidden_rows, axis=1)
        hidden_sum = hidden_sum + jnp.dot(columns, rows, preferred_element_type=jnp.float32)
    return jax.nn.relu(hidden_sum + mlp_bias[None, :]).astype(jnp.bfloat16)


def solution(mesh):
    in_specs = (
        P("tower", "feat", "groups", None),
        P("tower", "feat", "groups", None),
        P("tower", None),
        P("tower", "feat", None),
        P("tower", "feat", None),
        P("tower", None),
        P("tower", "feat", None),
        P("tower", None),
        P(("groups", "feat", "tower"), None),
        P("tower", None),
        P(),
    )
    out_specs = P(("groups", "feat", "tower"), None)
    body = functools.partial(
        on_device, feat_count=mesh.shape["feat"],
        group_count=mesh.shape["groups"],
        tower_count=mesh.shape["tower"],
    )
    return jax.shard_map(body, mesh=mesh, in_specs=in_specs, out_specs=out_specs, check_vma=False)
```

```python
import functools
import math

import jax
import jax.numpy as jnp
import numpy as np
from jax import lax
from jax.sharding import PartitionSpec as P


def pair_positions(vector_count):
    upper_rows, upper_cols = np.triu_indices(vector_count, 1)
    return upper_rows * vector_count + upper_cols


def weight_parts(weights_here, feat_count, group_count, share_count, entry_count):
    rows_here = weights_here.shape[0]
    piece = rows_here // share_count
    blocks_here = rows_here // entry_count
    blocks_piece = piece // entry_count
    owner = lax.axis_index("feat")
    group = lax.axis_index("groups") if share_count > 1 else 0
    block_range = jnp.arange(blocks_piece, dtype=jnp.int32)
    parts = [(weights_here, owner * blocks_here + jnp.arange(blocks_here, dtype=jnp.int32))]
    if share_count > 1:
        travelling = lax.dynamic_slice_in_dim(weights_here, group * piece, piece, axis=0)
    else:
        travelling = weights_here
    chunk_count = next(count for count in (4, 2, 1) if blocks_piece % count == 0)
    chunk_blocks = blocks_piece // chunk_count
    chunk_rows = chunk_blocks * entry_count
    chunk_range = jnp.arange(chunk_blocks, dtype=jnp.int32)
    rings = [
        lax.slice_in_dim(travelling, chunk * chunk_rows, (chunk + 1) * chunk_rows, axis=0)
        for chunk in range(chunk_count)
    ]
    ring = [(source, (source + 1) % feat_count) for source in range(feat_count)]
    for step in range(1, feat_count):
        source_block = (owner - step) % feat_count
        for chunk in range(chunk_count):
            rings[chunk] = lax.ppermute(rings[chunk], "feat", ring)
            first_block = source_block * blocks_here + chunk * chunk_blocks
            parts.append((rings[chunk], first_block + group * blocks_piece + chunk_range))
            for shift in range(1, share_count):
                pairs = [(source, (source + shift) % group_count) for source in range(group_count)]
                forwarded = lax.ppermute(rings[chunk], "groups", pairs)
                from_group = (group - shift) % group_count
                parts.append((forwarded, first_block + from_group * blocks_piece + chunk_range))
    travelling = rings
    return parts, travelling


def exchange_rows(first, second, feat_count):
    slots_here, row_count, _ = first.shape
    share = row_count // feat_count
    owner = lax.axis_index("feat")
    pieces, ids = [], []
    for shift in range(feat_count):
        target = (owner + shift) % feat_count
        piece = jnp.concatenate(
            [
                lax.dynamic_slice_in_dim(first, target * share, share, axis=1),
                lax.dynamic_slice_in_dim(second, target * share, share, axis=1),
            ],
            0,
        )
        if shift:
            piece = lax.ppermute(
                piece, "feat", [(source, (source + shift) % feat_count) for source in range(feat_count)]
            )
        source = (owner - shift) % feat_count
        local = jnp.arange(slots_here, dtype=jnp.int32)
        ids.append(
            jnp.concatenate([source * slots_here + local, (feat_count + source) * slots_here + local])
        )
        pieces.append(piece)
    return pieces, ids


def on_device(
    pooled_first,
    pooled_second,
    feature_order,
    cross_down,
    cross_up,
    cross_bias,
    compress_weight,
    compress_bias,
    dense_vector,
    mlp_weight,
    mlp_bias,
    *,
    feat_count,
    group_count,
    tower_count,
):
    entry_count = pooled_first.shape[3]
    rows_here = cross_down.shape[1]
    rank = cross_down.shape[2]
    split = rows_here % group_count == 0 and (rows_here // group_count) % entry_count == 0
    share_count = group_count if split else 1

    hidden_pieces = [mlp_weight]
    for shift in range(1, tower_count):
        pairs = [(source, (source + shift) % tower_count) for source in range(tower_count)]
        hidden_pieces.append(lax.ppermute(mlp_weight, "tower", pairs))

    weights_here = jnp.concatenate([cross_down[0], cross_up[0], compress_weight[0]], axis=1)
    parts, last_rows = weight_parts(weights_here, feat_count, group_count, share_count, entry_count)

    first_rows, second_rows, _ = lax.optimization_barrier(
        (pooled_first[0], pooled_second[0], last_rows)
    )
    pieces, slot_ids = exchange_rows(first_rows, second_rows, feat_count)
    row_count = pieces[0].shape[1]
    slot_count = sum(piece.shape[0] for piece in pieces)
    bias_blocks = cross_bias[0].reshape(slot_count, entry_count)
    features = jnp.concatenate([part_features for _, part_features in parts])
    position_count = features.shape[0]

    if len(pieces) > 4:
        pieces, slot_ids = [jnp.concatenate(pieces, 0)], [jnp.concatenate(slot_ids)]
    weights = jnp.concatenate([rows for rows, _ in parts], 0)
    base_all = None
    low_sum = None
    for piece, ids in zip(pieces, slot_ids):
        orders = feature_order[0][ids]
        one_hot = (orders[None, :] == features[:, None]).astype(jnp.bfloat16)
        term = jnp.einsum("fs,sre->rfe", one_hot, piece, preferred_element_type=jnp.bfloat16)
        term = term.reshape(row_count, position_count * entry_count)
        base_all = term if base_all is None else base_all + term
        partial = jnp.dot(term, weights[:, :rank], preferred_element_type=jnp.float32)
        low_sum = partial if low_sum is None else low_sum + partial
    low_rank = low_sum.astype(jnp.bfloat16)
    lifted = lax.dot_general(
        low_rank,
        weights[:, rank : 2 * rank],
        (((1,), (1,)), ((), ())),
        preferred_element_type=jnp.float32,
    )
    shift_row = bias_blocks[features].reshape(position_count * entry_count)
    columns = base_all.astype(jnp.float32)
    crossed = (columns * (lifted + shift_row[None, :]) + columns).astype(jnp.bfloat16)
    squeezed = jnp.dot(crossed, weights[:, 2 * rank :], preferred_element_type=jnp.float32)
    compressed = (squeezed + compress_bias[0][None, :]).astype(jnp.bfloat16)
    gathered = lax.all_to_all(compressed, "tower", split_axis=0, concat_axis=1, tiled=True)
    local_rows = gathered.shape[0]
    vector_count = gathered.shape[1] // entry_count
    vectors = gathered.reshape(local_rows, vector_count, entry_count)
    gram_matrix = jnp.einsum(
        "bie,bje->bij", vectors, vectors, preferred_element_type=jnp.float32
    ) * (1.0 / math.sqrt(entry_count))
    pair_terms = gram_matrix.reshape(local_rows, vector_count * vector_count)[
        :, pair_positions(vector_count)
    ]
    joined = jnp.concatenate([dense_vector.astype(jnp.float32), pair_terms], 1).astype(jnp.bfloat16)
    hidden_units = mlp_weight.shape[1]
    hidden_rows = mlp_weight.shape[0]
    tower = lax.axis_index("tower")
    hidden_sum = jnp.zeros((local_rows, hidden_units), jnp.float32)
    for shift, rows in enumerate(hidden_pieces):
        source = (tower - shift) % tower_count
        columns = lax.dynamic_slice_in_dim(joined, source * hidden_rows, hidden_rows, axis=1)
        hidden_sum = hidden_sum + jnp.dot(columns, rows, preferred_element_type=jnp.float32)
    return jax.nn.relu(hidden_sum + mlp_bias[None, :]).astype(jnp.bfloat16)


def solution(mesh):
    in_specs = (
        P("tower", "feat", "groups", None),
        P("tower", "feat", "groups", None),
        P("tower", None),
        P("tower", "feat", None),
        P("tower", "feat", None),
        P("tower", None),
        P("tower", "feat", None),
        P("tower", None),
        P(("groups", "feat", "tower"), None),
        P("tower", None),
        P(),
    )
    out_specs = P(("groups", "feat", "tower"), None)
    body = functools.partial(
        on_device, feat_count=mesh.shape["feat"],
        group_count=mesh.shape["groups"],
        tower_count=mesh.shape["tower"],
    )
    return jax.shard_map(body, mesh=mesh, in_specs=in_specs, out_specs=out_specs, check_vma=False)
```

```python
import functools
import math

import jax
import jax.numpy as jnp
import numpy as np
from jax import lax
from jax.sharding import PartitionSpec as P


def pair_positions(vector_count):
    upper_rows, upper_cols = np.triu_indices(vector_count, 1)
    return upper_rows * vector_count + upper_cols


def weight_parts(weights_here, feat_count, group_count, share_count, entry_count):
    rows_here = weights_here.shape[0]
    piece = rows_here // share_count
    blocks_here = rows_here // entry_count
    blocks_piece = piece // entry_count
    owner = lax.axis_index("feat")
    group = lax.axis_index("groups") if share_count > 1 else 0
    block_range = jnp.arange(blocks_piece, dtype=jnp.int32)
    parts = [(weights_here, owner * blocks_here + jnp.arange(blocks_here, dtype=jnp.int32))]
    if share_count > 1:
        travelling = lax.dynamic_slice_in_dim(weights_here, group * piece, piece, axis=0)
    else:
        travelling = weights_here
    chunk_count = next(count for count in (4, 2, 1) if blocks_piece % count == 0)
    chunk_blocks = blocks_piece // chunk_count
    chunk_rows = chunk_blocks * entry_count
    chunk_range = jnp.arange(chunk_blocks, dtype=jnp.int32)
    rings = [
        lax.slice_in_dim(travelling, chunk * chunk_rows, (chunk + 1) * chunk_rows, axis=0)
        for chunk in range(chunk_count)
    ]
    ring = [(source, (source + 1) % feat_count) for source in range(feat_count)]
    for step in range(1, feat_count):
        source_block = (owner - step) % feat_count
        for chunk in range(chunk_count):
            rings[chunk] = lax.ppermute(rings[chunk], "feat", ring)
            first_block = source_block * blocks_here + chunk * chunk_blocks
            parts.append((rings[chunk], first_block + group * blocks_piece + chunk_range))
            for shift in range(1, share_count):
                pairs = [(source, (source + shift) % group_count) for source in range(group_count)]
                forwarded = lax.ppermute(rings[chunk], "groups", pairs)
                from_group = (group - shift) % group_count
                parts.append((forwarded, first_block + from_group * blocks_piece + chunk_range))
    travelling = rings
    return parts, travelling


def exchange_rows(first, second, feat_count):
    slots_here, row_count, _ = first.shape
    share = row_count // feat_count
    owner = lax.axis_index("feat")
    pieces, ids = [], []
    for shift in range(feat_count):
        target = (owner + shift) % feat_count
        piece = jnp.concatenate(
            [
                lax.dynamic_slice_in_dim(first, target * share, share, axis=1),
                lax.dynamic_slice_in_dim(second, target * share, share, axis=1),
            ],
            0,
        )
        if shift:
            piece = lax.ppermute(
                piece, "feat", [(source, (source + shift) % feat_count) for source in range(feat_count)]
            )
        source = (owner - shift) % feat_count
        local = jnp.arange(slots_here, dtype=jnp.int32)
        ids.append(
            jnp.concatenate([source * slots_here + local, (feat_count + source) * slots_here + local])
        )
        pieces.append(piece)
    return pieces, ids


def on_device(
    pooled_first,
    pooled_second,
    feature_order,
    cross_down,
    cross_up,
    cross_bias,
    compress_weight,
    compress_bias,
    dense_vector,
    mlp_weight,
    mlp_bias,
    *,
    feat_count,
    group_count,
    tower_count,
):
    entry_count = pooled_first.shape[3]
    rows_here = cross_down.shape[1]
    rank = cross_down.shape[2]
    split = rows_here % group_count == 0 and (rows_here // group_count) % entry_count == 0
    share_count = group_count if split else 1

    hidden_pieces = [mlp_weight]
    for shift in range(1, tower_count):
        pairs = [(source, (source + shift) % tower_count) for source in range(tower_count)]
        hidden_pieces.append(lax.ppermute(mlp_weight, "tower", pairs))

    weights_here = jnp.concatenate([cross_down[0], cross_up[0], compress_weight[0]], axis=1)
    parts, last_rows = weight_parts(weights_here, feat_count, group_count, share_count, entry_count)

    first_rows, second_rows, _ = lax.optimization_barrier(
        (pooled_first[0], pooled_second[0], last_rows)
    )
    pieces, slot_ids = exchange_rows(first_rows, second_rows, feat_count)
    row_count = pieces[0].shape[1]
    slot_count = sum(piece.shape[0] for piece in pieces)
    bias_blocks = cross_bias[0].reshape(slot_count, entry_count)
    features = jnp.concatenate([part_features for _, part_features in parts])
    position_count = features.shape[0]

    if len(pieces) > 4:
        pieces, slot_ids = [jnp.concatenate(pieces, 0)], [jnp.concatenate(slot_ids)]
    weights = jnp.concatenate([rows for rows, _ in parts], 0)
    base_all = None
    low_sum = None
    for piece, ids in zip(pieces, slot_ids):
        orders = feature_order[0][ids]
        one_hot = (orders[None, :] == features[:, None]).astype(jnp.bfloat16)
        term = jnp.einsum("fs,sre->rfe", one_hot, piece, preferred_element_type=jnp.bfloat16)
        term = term.reshape(row_count, position_count * entry_count)
        base_all = term if base_all is None else base_all + term
        partial = jnp.dot(term, weights[:, :rank], preferred_element_type=jnp.float32)
        low_sum = partial if low_sum is None else low_sum + partial
    base_all, low_sum = lax.optimization_barrier((base_all, low_sum))
    low_rank = low_sum.astype(jnp.bfloat16)
    lifted = lax.dot_general(
        low_rank,
        weights[:, rank : 2 * rank],
        (((1,), (1,)), ((), ())),
        preferred_element_type=jnp.float32,
    )
    shift_row = bias_blocks[features].reshape(position_count * entry_count)
    columns = base_all.astype(jnp.float32)
    crossed = (columns * (lifted + shift_row[None, :]) + columns).astype(jnp.bfloat16)
    squeezed = jnp.dot(crossed, weights[:, 2 * rank :], preferred_element_type=jnp.float32)
    compressed = (squeezed + compress_bias[0][None, :]).astype(jnp.bfloat16)
    gathered = lax.all_to_all(compressed, "tower", split_axis=0, concat_axis=1, tiled=True)
    local_rows = gathered.shape[0]
    vector_count = gathered.shape[1] // entry_count
    vectors = gathered.reshape(local_rows, vector_count, entry_count)
    gram_matrix = jnp.einsum(
        "bie,bje->bij", vectors, vectors, preferred_element_type=jnp.float32
    ) * (1.0 / math.sqrt(entry_count))
    pair_terms = gram_matrix.reshape(local_rows, vector_count * vector_count)[
        :, pair_positions(vector_count)
    ]
    joined = jnp.concatenate([dense_vector.astype(jnp.float32), pair_terms], 1).astype(jnp.bfloat16)
    hidden_units = mlp_weight.shape[1]
    hidden_rows = mlp_weight.shape[0]
    tower = lax.axis_index("tower")
    hidden_sum = jnp.zeros((local_rows, hidden_units), jnp.float32)
    for shift, rows in enumerate(hidden_pieces):
        source = (tower - shift) % tower_count
        columns = lax.dynamic_slice_in_dim(joined, source * hidden_rows, hidden_rows, axis=1)
        hidden_sum = hidden_sum + jnp.dot(columns, rows, preferred_element_type=jnp.float32)
    return jax.nn.relu(hidden_sum + mlp_bias[None, :]).astype(jnp.bfloat16)


def solution(mesh):
    in_specs = (
        P("tower", "feat", "groups", None),
        P("tower", "feat", "groups", None),
        P("tower", None),
        P("tower", "feat", None),
        P("tower", "feat", None),
        P("tower", None),
        P("tower", "feat", None),
        P("tower", None),
        P(("groups", "feat", "tower"), None),
        P("tower", None),
        P(),
    )
    out_specs = P(("groups", "feat", "tower"), None)
    body = functools.partial(
        on_device, feat_count=mesh.shape["feat"],
        group_count=mesh.shape["groups"],
        tower_count=mesh.shape["tower"],
    )
    return jax.shard_map(body, mesh=mesh, in_specs=in_specs, out_specs=out_specs, check_vma=False)
```

```python
import functools
import math

import jax
import jax.numpy as jnp
import numpy as np
from jax import lax
from jax.sharding import PartitionSpec as P


def pair_positions(vector_count):
    upper_rows, upper_cols = np.triu_indices(vector_count, 1)
    return upper_rows * vector_count + upper_cols


def weight_parts(weights_here, feat_count, group_count, share_count, entry_count):
    rows_here = weights_here.shape[0]
    piece = rows_here // share_count
    blocks_here = rows_here // entry_count
    blocks_piece = piece // entry_count
    owner = lax.axis_index("feat")
    group = lax.axis_index("groups") if share_count > 1 else 0
    block_range = jnp.arange(blocks_piece, dtype=jnp.int32)
    parts = [(weights_here, owner * blocks_here + jnp.arange(blocks_here, dtype=jnp.int32))]
    if share_count > 1:
        travelling = lax.dynamic_slice_in_dim(weights_here, group * piece, piece, axis=0)
    else:
        travelling = weights_here
    chunk_count = next(count for count in (4, 2, 1) if blocks_piece % count == 0)
    chunk_blocks = blocks_piece // chunk_count
    chunk_rows = chunk_blocks * entry_count
    chunk_range = jnp.arange(chunk_blocks, dtype=jnp.int32)
    rings = [
        lax.slice_in_dim(travelling, chunk * chunk_rows, (chunk + 1) * chunk_rows, axis=0)
        for chunk in range(chunk_count)
    ]
    ring = [(source, (source + 1) % feat_count) for source in range(feat_count)]
    for step in range(1, feat_count):
        source_block = (owner - step) % feat_count
        for chunk in range(chunk_count):
            rings[chunk] = lax.ppermute(rings[chunk], "feat", ring)
            first_block = source_block * blocks_here + chunk * chunk_blocks
            parts.append((rings[chunk], first_block + group * blocks_piece + chunk_range))
            for shift in range(1, share_count):
                pairs = [(source, (source + shift) % group_count) for source in range(group_count)]
                forwarded = lax.ppermute(rings[chunk], "groups", pairs)
                from_group = (group - shift) % group_count
                parts.append((forwarded, first_block + from_group * blocks_piece + chunk_range))
    travelling = rings
    return parts, travelling


def exchange_rows(first, second, feat_count):
    slots_here, row_count, _ = first.shape
    share = row_count // feat_count
    owner = lax.axis_index("feat")
    pieces, ids = [], []
    for shift in range(feat_count):
        target = (owner + shift) % feat_count
        piece = jnp.concatenate(
            [
                lax.dynamic_slice_in_dim(first, target * share, share, axis=1),
                lax.dynamic_slice_in_dim(second, target * share, share, axis=1),
            ],
            0,
        )
        if shift:
            piece = lax.ppermute(
                piece, "feat", [(source, (source + shift) % feat_count) for source in range(feat_count)]
            )
        source = (owner - shift) % feat_count
        local = jnp.arange(slots_here, dtype=jnp.int32)
        ids.append(
            jnp.concatenate([source * slots_here + local, (feat_count + source) * slots_here + local])
        )
        pieces.append(piece)
    return pieces, ids


def on_device(
    pooled_first,
    pooled_second,
    feature_order,
    cross_down,
    cross_up,
    cross_bias,
    compress_weight,
    compress_bias,
    dense_vector,
    mlp_weight,
    mlp_bias,
    *,
    feat_count,
    group_count,
    tower_count,
):
    entry_count = pooled_first.shape[3]
    rows_here = cross_down.shape[1]
    rank = cross_down.shape[2]
    split = rows_here % group_count == 0 and (rows_here // group_count) % entry_count == 0
    share_count = group_count if split else 1

    hidden_pieces = [mlp_weight]
    for shift in range(1, tower_count):
        pairs = [(source, (source + shift) % tower_count) for source in range(tower_count)]
        hidden_pieces.append(lax.ppermute(mlp_weight, "tower", pairs))

    weights_here = jnp.concatenate([cross_down[0], cross_up[0], compress_weight[0]], axis=1)
    parts, last_rows = weight_parts(weights_here, feat_count, group_count, share_count, entry_count)

    first_rows, second_rows, _ = lax.optimization_barrier(
        (pooled_first[0], pooled_second[0], (last_rows, hidden_pieces))
    )
    pieces, slot_ids = exchange_rows(first_rows, second_rows, feat_count)
    row_count = pieces[0].shape[1]
    slot_count = sum(piece.shape[0] for piece in pieces)
    bias_blocks = cross_bias[0].reshape(slot_count, entry_count)
    features = jnp.concatenate([part_features for _, part_features in parts])
    position_count = features.shape[0]

    if len(pieces) > 4:
        pieces, slot_ids = [jnp.concatenate(pieces, 0)], [jnp.concatenate(slot_ids)]
    weights = jnp.concatenate([rows for rows, _ in parts], 0)
    base_all = None
    low_sum = None
    for piece, ids in zip(pieces, slot_ids):
        orders = feature_order[0][ids]
        one_hot = (orders[None, :] == features[:, None]).astype(jnp.bfloat16)
        term = jnp.einsum("fs,sre->rfe", one_hot, piece, preferred_element_type=jnp.bfloat16)
        term = term.reshape(row_count, position_count * entry_count)
        base_all = term if base_all is None else base_all + term
        partial = jnp.dot(term, weights[:, :rank], preferred_element_type=jnp.float32)
        low_sum = partial if low_sum is None else low_sum + partial
    base_all, low_sum = lax.optimization_barrier((base_all, low_sum))
    low_rank = low_sum.astype(jnp.bfloat16)
    lifted = lax.dot_general(
        low_rank,
        weights[:, rank : 2 * rank],
        (((1,), (1,)), ((), ())),
        preferred_element_type=jnp.float32,
    )
    shift_row = bias_blocks[features].reshape(position_count * entry_count)
    columns = base_all.astype(jnp.float32)
    crossed = (columns * (lifted + shift_row[None, :]) + columns).astype(jnp.bfloat16)
    squeezed = jnp.dot(crossed, weights[:, 2 * rank :], preferred_element_type=jnp.float32)
    compressed = (squeezed + compress_bias[0][None, :]).astype(jnp.bfloat16)
    gathered = lax.all_to_all(compressed, "tower", split_axis=0, concat_axis=1, tiled=True)
    local_rows = gathered.shape[0]
    vector_count = gathered.shape[1] // entry_count
    vectors = gathered.reshape(local_rows, vector_count, entry_count)
    gram_matrix = jnp.einsum(
        "bie,bje->bij", vectors, vectors, preferred_element_type=jnp.float32
    ) * (1.0 / math.sqrt(entry_count))
    pair_terms = gram_matrix.reshape(local_rows, vector_count * vector_count)[
        :, pair_positions(vector_count)
    ]
    joined = jnp.concatenate([dense_vector.astype(jnp.float32), pair_terms], 1).astype(jnp.bfloat16)
    hidden_units = mlp_weight.shape[1]
    hidden_rows = mlp_weight.shape[0]
    tower = lax.axis_index("tower")
    hidden_sum = jnp.zeros((local_rows, hidden_units), jnp.float32)
    for shift, rows in enumerate(hidden_pieces):
        source = (tower - shift) % tower_count
        columns = lax.dynamic_slice_in_dim(joined, source * hidden_rows, hidden_rows, axis=1)
        hidden_sum = hidden_sum + jnp.dot(columns, rows, preferred_element_type=jnp.float32)
    return jax.nn.relu(hidden_sum + mlp_bias[None, :]).astype(jnp.bfloat16)


def solution(mesh):
    in_specs = (
        P("tower", "feat", "groups", None),
        P("tower", "feat", "groups", None),
        P("tower", None),
        P("tower", "feat", None),
        P("tower", "feat", None),
        P("tower", None),
        P("tower", "feat", None),
        P("tower", None),
        P(("groups", "feat", "tower"), None),
        P("tower", None),
        P(),
    )
    out_specs = P(("groups", "feat", "tower"), None)
    body = functools.partial(
        on_device, feat_count=mesh.shape["feat"],
        group_count=mesh.shape["groups"],
        tower_count=mesh.shape["tower"],
    )
    return jax.shard_map(body, mesh=mesh, in_specs=in_specs, out_specs=out_specs, check_vma=False)
```

```python
import functools
import math

import jax
import jax.numpy as jnp
import numpy as np
from jax import lax
from jax.sharding import PartitionSpec as P


def pair_positions(vector_count):
    upper_rows, upper_cols = np.triu_indices(vector_count, 1)
    return upper_rows * vector_count + upper_cols


def weight_parts(weights_here, feat_count, group_count, share_count, entry_count):
    rows_here = weights_here.shape[0]
    piece = rows_here // share_count
    blocks_here = rows_here // entry_count
    blocks_piece = piece // entry_count
    owner = lax.axis_index("feat")
    group = lax.axis_index("groups") if share_count > 1 else 0
    block_range = jnp.arange(blocks_piece, dtype=jnp.int32)
    parts = [(weights_here, owner * blocks_here + jnp.arange(blocks_here, dtype=jnp.int32))]
    if share_count > 1:
        travelling = lax.dynamic_slice_in_dim(weights_here, group * piece, piece, axis=0)
    else:
        travelling = weights_here
    chunk_count = next(count for count in (4, 2, 1) if blocks_piece % count == 0)
    chunk_blocks = blocks_piece // chunk_count
    chunk_rows = chunk_blocks * entry_count
    chunk_range = jnp.arange(chunk_blocks, dtype=jnp.int32)
    rings = [
        lax.slice_in_dim(travelling, chunk * chunk_rows, (chunk + 1) * chunk_rows, axis=0)
        for chunk in range(chunk_count)
    ]
    ring = [(source, (source + 1) % feat_count) for source in range(feat_count)]
    for step in range(1, feat_count):
        source_block = (owner - step) % feat_count
        for chunk in range(chunk_count):
            rings[chunk] = lax.ppermute(rings[chunk], "feat", ring)
            first_block = source_block * blocks_here + chunk * chunk_blocks
            parts.append((rings[chunk], first_block + group * blocks_piece + chunk_range))
            for shift in range(1, share_count):
                pairs = [(source, (source + shift) % group_count) for source in range(group_count)]
                forwarded = lax.ppermute(rings[chunk], "groups", pairs)
                from_group = (group - shift) % group_count
                parts.append((forwarded, first_block + from_group * blocks_piece + chunk_range))
    travelling = rings
    return parts, travelling


def exchange_rows(first, second, feat_count):
    slots_here, row_count, _ = first.shape
    share = row_count // feat_count
    owner = lax.axis_index("feat")
    pieces, ids = [], []
    for shift in range(feat_count):
        target = (owner + shift) % feat_count
        piece = jnp.concatenate(
            [
                lax.dynamic_slice_in_dim(first, target * share, share, axis=1),
                lax.dynamic_slice_in_dim(second, target * share, share, axis=1),
            ],
            0,
        )
        if shift:
            piece = lax.ppermute(
                piece, "feat", [(source, (source + shift) % feat_count) for source in range(feat_count)]
            )
        source = (owner - shift) % feat_count
        local = jnp.arange(slots_here, dtype=jnp.int32)
        ids.append(
            jnp.concatenate([source * slots_here + local, (feat_count + source) * slots_here + local])
        )
        pieces.append(piece)
    return pieces, ids


def on_device(
    pooled_first,
    pooled_second,
    feature_order,
    cross_down,
    cross_up,
    cross_bias,
    compress_weight,
    compress_bias,
    dense_vector,
    mlp_weight,
    mlp_bias,
    *,
    feat_count,
    group_count,
    tower_count,
):
    entry_count = pooled_first.shape[3]
    rows_here = cross_down.shape[1]
    rank = cross_down.shape[2]
    split = rows_here % group_count == 0 and (rows_here // group_count) % entry_count == 0
    share_count = group_count if split else 1

    hidden_pieces = [mlp_weight]
    for shift in range(1, tower_count):
        pairs = [(source, (source + shift) % tower_count) for source in range(tower_count)]
        hidden_pieces.append(lax.ppermute(mlp_weight, "tower", pairs))

    weights_here = jnp.concatenate([cross_down[0], cross_up[0], compress_weight[0]], axis=1)
    parts, last_rows = weight_parts(weights_here, feat_count, group_count, share_count, entry_count)

    first_rows, second_rows, _ = lax.optimization_barrier(
        (pooled_first[0], pooled_second[0], last_rows[: max(1, len(last_rows) - 1)])
    )
    pieces, slot_ids = exchange_rows(first_rows, second_rows, feat_count)
    row_count = pieces[0].shape[1]
    slot_count = sum(piece.shape[0] for piece in pieces)
    bias_blocks = cross_bias[0].reshape(slot_count, entry_count)
    features = jnp.concatenate([part_features for _, part_features in parts])
    position_count = features.shape[0]

    if len(pieces) > 4:
        pieces, slot_ids = [jnp.concatenate(pieces, 0)], [jnp.concatenate(slot_ids)]
    base_sum = None
    for piece, ids in zip(pieces, slot_ids):
        orders = feature_order[0][ids]
        one_hot = (orders[None, :] == features[:, None]).astype(jnp.bfloat16)
        term = jnp.einsum("fs,sre->rfe", one_hot, piece, preferred_element_type=jnp.float32)
        base_sum = term if base_sum is None else base_sum + term
    base_all = base_sum.astype(jnp.bfloat16).reshape(row_count, position_count * entry_count)

    weights = jnp.concatenate([rows for rows, _ in parts], 0)
    low_sum = jnp.dot(base_all, weights[:, :rank], preferred_element_type=jnp.float32)
    low_rank = low_sum.astype(jnp.bfloat16)
    lifted = lax.dot_general(
        low_rank,
        weights[:, rank : 2 * rank],
        (((1,), (1,)), ((), ())),
        preferred_element_type=jnp.float32,
    )
    shift_row = bias_blocks[features].reshape(position_count * entry_count)
    columns = base_all.astype(jnp.float32)
    crossed = (columns * (lifted + shift_row[None, :]) + columns).astype(jnp.bfloat16)
    squeezed = jnp.dot(crossed, weights[:, 2 * rank :], preferred_element_type=jnp.float32)
    compressed = (squeezed + compress_bias[0][None, :]).astype(jnp.bfloat16)
    gathered = lax.all_to_all(compressed, "tower", split_axis=0, concat_axis=1, tiled=True)
    local_rows = gathered.shape[0]
    vector_count = gathered.shape[1] // entry_count
    vectors = gathered.reshape(local_rows, vector_count, entry_count)
    gram_matrix = jnp.einsum(
        "bie,bje->bij", vectors, vectors, preferred_element_type=jnp.float32
    ) * (1.0 / math.sqrt(entry_count))
    pair_terms = gram_matrix.reshape(local_rows, vector_count * vector_count)[
        :, pair_positions(vector_count)
    ]
    joined = jnp.concatenate([dense_vector.astype(jnp.float32), pair_terms], 1).astype(jnp.bfloat16)
    hidden_units = mlp_weight.shape[1]
    hidden_rows = mlp_weight.shape[0]
    tower = lax.axis_index("tower")
    hidden_sum = jnp.zeros((local_rows, hidden_units), jnp.float32)
    for shift, rows in enumerate(hidden_pieces):
        source = (tower - shift) % tower_count
        columns = lax.dynamic_slice_in_dim(joined, source * hidden_rows, hidden_rows, axis=1)
        hidden_sum = hidden_sum + jnp.dot(columns, rows, preferred_element_type=jnp.float32)
    return jax.nn.relu(hidden_sum + mlp_bias[None, :]).astype(jnp.bfloat16)


def solution(mesh):
    in_specs = (
        P("tower", "feat", "groups", None),
        P("tower", "feat", "groups", None),
        P("tower", None),
        P("tower", "feat", None),
        P("tower", "feat", None),
        P("tower", None),
        P("tower", "feat", None),
        P("tower", None),
        P(("groups", "feat", "tower"), None),
        P("tower", None),
        P(),
    )
    out_specs = P(("groups", "feat", "tower"), None)
    body = functools.partial(
        on_device, feat_count=mesh.shape["feat"],
        group_count=mesh.shape["groups"],
        tower_count=mesh.shape["tower"],
    )
    return jax.shard_map(body, mesh=mesh, in_specs=in_specs, out_specs=out_specs, check_vma=False)
```

```python
import functools
import math

import jax
import jax.numpy as jnp
import numpy as np
from jax import lax
from jax.sharding import PartitionSpec as P


def pair_positions(vector_count):
    upper_rows, upper_cols = np.triu_indices(vector_count, 1)
    return upper_rows * vector_count + upper_cols


def weight_parts(weights_here, feat_count, group_count, share_count, entry_count):
    rows_here = weights_here.shape[0]
    piece = rows_here // share_count
    blocks_here = rows_here // entry_count
    blocks_piece = piece // entry_count
    owner = lax.axis_index("feat")
    group = lax.axis_index("groups") if share_count > 1 else 0
    block_range = jnp.arange(blocks_piece, dtype=jnp.int32)
    parts = [(weights_here, owner * blocks_here + jnp.arange(blocks_here, dtype=jnp.int32))]
    if share_count > 1:
        travelling = lax.dynamic_slice_in_dim(weights_here, group * piece, piece, axis=0)
    else:
        travelling = weights_here
    chunk_count = next(count for count in (4, 2, 1) if blocks_piece % count == 0)
    chunk_blocks = blocks_piece // chunk_count
    chunk_rows = chunk_blocks * entry_count
    chunk_range = jnp.arange(chunk_blocks, dtype=jnp.int32)
    rings = [
        lax.slice_in_dim(travelling, chunk * chunk_rows, (chunk + 1) * chunk_rows, axis=0)
        for chunk in range(chunk_count)
    ]
    ring = [(source, (source + 1) % feat_count) for source in range(feat_count)]
    for step in range(1, feat_count):
        source_block = (owner - step) % feat_count
        for chunk in range(chunk_count):
            rings[chunk] = lax.ppermute(rings[chunk], "feat", ring)
            first_block = source_block * blocks_here + chunk * chunk_blocks
            parts.append((rings[chunk], first_block + group * blocks_piece + chunk_range))
        arrived = jnp.concatenate(rings, 0) if chunk_count > 1 else rings[0]
        for shift in range(1, share_count):
            pairs = [(source, (source + shift) % group_count) for source in range(group_count)]
            forwarded = lax.ppermute(arrived, "groups", pairs)
            from_group = (group - shift) % group_count
            parts.append((forwarded, source_block * blocks_here + from_group * blocks_piece + block_range))
    travelling = rings
    return parts, travelling


def exchange_rows(first, second, feat_count):
    slots_here, row_count, _ = first.shape
    share = row_count // feat_count
    owner = lax.axis_index("feat")
    pieces, ids = [], []
    for shift in range(feat_count):
        target = (owner + shift) % feat_count
        piece = jnp.concatenate(
            [
                lax.dynamic_slice_in_dim(first, target * share, share, axis=1),
                lax.dynamic_slice_in_dim(second, target * share, share, axis=1),
            ],
            0,
        )
        if shift:
            piece = lax.ppermute(
                piece, "feat", [(source, (source + shift) % feat_count) for source in range(feat_count)]
            )
        source = (owner - shift) % feat_count
        local = jnp.arange(slots_here, dtype=jnp.int32)
        ids.append(
            jnp.concatenate([source * slots_here + local, (feat_count + source) * slots_here + local])
        )
        pieces.append(piece)
    return pieces, ids


def on_device(
    pooled_first,
    pooled_second,
    feature_order,
    cross_down,
    cross_up,
    cross_bias,
    compress_weight,
    compress_bias,
    dense_vector,
    mlp_weight,
    mlp_bias,
    *,
    feat_count,
    group_count,
    tower_count,
):
    entry_count = pooled_first.shape[3]
    rows_here = cross_down.shape[1]
    rank = cross_down.shape[2]
    split = rows_here % group_count == 0 and (rows_here // group_count) % entry_count == 0
    share_count = group_count if split else 1

    hidden_pieces = [mlp_weight]
    for shift in range(1, tower_count):
        pairs = [(source, (source + shift) % tower_count) for source in range(tower_count)]
        hidden_pieces.append(lax.ppermute(mlp_weight, "tower", pairs))

    weights_here = jnp.concatenate([cross_down[0], cross_up[0], compress_weight[0]], axis=1)
    parts, last_rows = weight_parts(weights_here, feat_count, group_count, share_count, entry_count)

    first_rows, second_rows, _ = lax.optimization_barrier(
        (pooled_first[0], pooled_second[0], last_rows)
    )
    pieces, slot_ids = exchange_rows(first_rows, second_rows, feat_count)
    row_count = pieces[0].shape[1]
    slot_count = sum(piece.shape[0] for piece in pieces)
    bias_blocks = cross_bias[0].reshape(slot_count, entry_count)
    features = jnp.concatenate([part_features for _, part_features in parts])
    position_count = features.shape[0]

    if len(pieces) > 4:
        pieces, slot_ids = [jnp.concatenate(pieces, 0)], [jnp.concatenate(slot_ids)]
    base_sum = None
    for piece, ids in zip(pieces, slot_ids):
        orders = feature_order[0][ids]
        one_hot = (orders[None, :] == features[:, None]).astype(jnp.bfloat16)
        term = jnp.einsum("fs,sre->rfe", one_hot, piece, preferred_element_type=jnp.float32)
        base_sum = term if base_sum is None else base_sum + term
    base_all = base_sum.astype(jnp.bfloat16).reshape(row_count, position_count * entry_count)

    weights = jnp.concatenate([rows for rows, _ in parts], 0)
    low_sum = jnp.dot(base_all, weights[:, :rank], preferred_element_type=jnp.float32)
    low_rank = low_sum.astype(jnp.bfloat16)
    lifted = lax.dot_general(
        low_rank,
        weights[:, rank : 2 * rank],
        (((1,), (1,)), ((), ())),
        preferred_element_type=jnp.float32,
    )
    shift_row = bias_blocks[features].reshape(position_count * entry_count)
    columns = base_all.astype(jnp.float32)
    crossed = (columns * (lifted + shift_row[None, :]) + columns).astype(jnp.bfloat16)
    squeezed = jnp.dot(crossed, weights[:, 2 * rank :], preferred_element_type=jnp.float32)
    compressed = (squeezed + compress_bias[0][None, :]).astype(jnp.bfloat16)
    gathered = lax.all_to_all(compressed, "tower", split_axis=0, concat_axis=1, tiled=True)
    local_rows = gathered.shape[0]
    vector_count = gathered.shape[1] // entry_count
    vectors = gathered.reshape(local_rows, vector_count, entry_count)
    gram_matrix = jnp.einsum(
        "bie,bje->bij", vectors, vectors, preferred_element_type=jnp.float32
    ) * (1.0 / math.sqrt(entry_count))
    pair_terms = gram_matrix.reshape(local_rows, vector_count * vector_count)[
        :, pair_positions(vector_count)
    ]
    joined = jnp.concatenate([dense_vector.astype(jnp.float32), pair_terms], 1).astype(jnp.bfloat16)
    hidden_units = mlp_weight.shape[1]
    hidden_rows = mlp_weight.shape[0]
    tower = lax.axis_index("tower")
    hidden_sum = jnp.zeros((local_rows, hidden_units), jnp.float32)
    for shift, rows in enumerate(hidden_pieces):
        source = (tower - shift) % tower_count
        columns = lax.dynamic_slice_in_dim(joined, source * hidden_rows, hidden_rows, axis=1)
        hidden_sum = hidden_sum + jnp.dot(columns, rows, preferred_element_type=jnp.float32)
    return jax.nn.relu(hidden_sum + mlp_bias[None, :]).astype(jnp.bfloat16)


def solution(mesh):
    in_specs = (
        P("tower", "feat", "groups", None),
        P("tower", "feat", "groups", None),
        P("tower", None),
        P("tower", "feat", None),
        P("tower", "feat", None),
        P("tower", None),
        P("tower", "feat", None),
        P("tower", None),
        P(("groups", "feat", "tower"), None),
        P("tower", None),
        P(),
    )
    out_specs = P(("groups", "feat", "tower"), None)
    body = functools.partial(
        on_device, feat_count=mesh.shape["feat"],
        group_count=mesh.shape["groups"],
        tower_count=mesh.shape["tower"],
    )
    return jax.shard_map(body, mesh=mesh, in_specs=in_specs, out_specs=out_specs, check_vma=False)
```

```python
import functools
import math

import jax
import jax.numpy as jnp
import numpy as np
from jax import lax
from jax.sharding import PartitionSpec as P


def pair_positions(vector_count):
    upper_rows, upper_cols = np.triu_indices(vector_count, 1)
    return upper_rows * vector_count + upper_cols


def weight_parts(weights_here, feat_count, group_count, share_count, entry_count):
    rows_here = weights_here.shape[0]
    piece = rows_here // share_count
    blocks_here = rows_here // entry_count
    blocks_piece = piece // entry_count
    owner = lax.axis_index("feat")
    group = lax.axis_index("groups") if share_count > 1 else 0
    block_range = jnp.arange(blocks_piece, dtype=jnp.int32)
    parts = [(weights_here, owner * blocks_here + jnp.arange(blocks_here, dtype=jnp.int32))]
    if share_count > 1:
        travelling = lax.dynamic_slice_in_dim(weights_here, group * piece, piece, axis=0)
    else:
        travelling = weights_here
    chunk_count = next(count for count in (4, 2, 1) if blocks_piece % count == 0)
    chunk_blocks = blocks_piece // chunk_count
    chunk_rows = chunk_blocks * entry_count
    chunk_range = jnp.arange(chunk_blocks, dtype=jnp.int32)
    rings = [
        lax.slice_in_dim(travelling, chunk * chunk_rows, (chunk + 1) * chunk_rows, axis=0)
        for chunk in range(chunk_count)
    ]
    for step in range(1, feat_count):
        for chunk in range(chunk_count):
            way = 1 if chunk % 2 == 0 else -1
            ring = [(source, (source + way) % feat_count) for source in range(feat_count)]
            source_block = (owner - way * step) % feat_count
            rings[chunk] = lax.ppermute(rings[chunk], "feat", ring)
            first_block = source_block * blocks_here + chunk * chunk_blocks
            parts.append((rings[chunk], first_block + group * blocks_piece + chunk_range))
            for shift in range(1, share_count):
                pairs = [(source, (source + shift) % group_count) for source in range(group_count)]
                forwarded = lax.ppermute(rings[chunk], "groups", pairs)
                from_group = (group - shift) % group_count
                parts.append((forwarded, first_block + from_group * blocks_piece + chunk_range))
    travelling = rings
    return parts, travelling


def exchange_rows(first, second, feat_count):
    slots_here, row_count, _ = first.shape
    share = row_count // feat_count
    owner = lax.axis_index("feat")
    pieces, ids = [], []
    for shift in range(feat_count):
        target = (owner + shift) % feat_count
        piece = jnp.concatenate(
            [
                lax.dynamic_slice_in_dim(first, target * share, share, axis=1),
                lax.dynamic_slice_in_dim(second, target * share, share, axis=1),
            ],
            0,
        )
        if shift:
            piece = lax.ppermute(
                piece, "feat", [(source, (source + shift) % feat_count) for source in range(feat_count)]
            )
        source = (owner - shift) % feat_count
        local = jnp.arange(slots_here, dtype=jnp.int32)
        ids.append(
            jnp.concatenate([source * slots_here + local, (feat_count + source) * slots_here + local])
        )
        pieces.append(piece)
    return pieces, ids


def on_device(
    pooled_first,
    pooled_second,
    feature_order,
    cross_down,
    cross_up,
    cross_bias,
    compress_weight,
    compress_bias,
    dense_vector,
    mlp_weight,
    mlp_bias,
    *,
    feat_count,
    group_count,
    tower_count,
):
    entry_count = pooled_first.shape[3]
    rows_here = cross_down.shape[1]
    rank = cross_down.shape[2]
    split = rows_here % group_count == 0 and (rows_here // group_count) % entry_count == 0
    share_count = group_count if split else 1

    hidden_pieces = [mlp_weight]
    for shift in range(1, tower_count):
        pairs = [(source, (source + shift) % tower_count) for source in range(tower_count)]
        hidden_pieces.append(lax.ppermute(mlp_weight, "tower", pairs))

    weights_here = jnp.concatenate([cross_down[0], cross_up[0], compress_weight[0]], axis=1)
    parts, last_rows = weight_parts(weights_here, feat_count, group_count, share_count, entry_count)

    first_rows, second_rows, _ = lax.optimization_barrier(
        (pooled_first[0], pooled_second[0], last_rows)
    )
    pieces, slot_ids = exchange_rows(first_rows, second_rows, feat_count)
    row_count = pieces[0].shape[1]
    slot_count = sum(piece.shape[0] for piece in pieces)
    bias_blocks = cross_bias[0].reshape(slot_count, entry_count)
    features = jnp.concatenate([part_features for _, part_features in parts])
    position_count = features.shape[0]

    if len(pieces) > 4:
        pieces, slot_ids = [jnp.concatenate(pieces, 0)], [jnp.concatenate(slot_ids)]
    base_sum = None
    for piece, ids in zip(pieces, slot_ids):
        orders = feature_order[0][ids]
        one_hot = (orders[None, :] == features[:, None]).astype(jnp.bfloat16)
        term = jnp.einsum("fs,sre->rfe", one_hot, piece, preferred_element_type=jnp.float32)
        base_sum = term if base_sum is None else base_sum + term
    base_all = base_sum.astype(jnp.bfloat16).reshape(row_count, position_count * entry_count)

    weights = jnp.concatenate([rows for rows, _ in parts], 0)
    low_sum = jnp.dot(base_all, weights[:, :rank], preferred_element_type=jnp.float32)
    low_rank = low_sum.astype(jnp.bfloat16)
    lifted = lax.dot_general(
        low_rank,
        weights[:, rank : 2 * rank],
        (((1,), (1,)), ((), ())),
        preferred_element_type=jnp.float32,
    )
    shift_row = bias_blocks[features].reshape(position_count * entry_count)
    columns = base_all.astype(jnp.float32)
    crossed = (columns * (lifted + shift_row[None, :]) + columns).astype(jnp.bfloat16)
    squeezed = jnp.dot(crossed, weights[:, 2 * rank :], preferred_element_type=jnp.float32)
    compressed = (squeezed + compress_bias[0][None, :]).astype(jnp.bfloat16)
    gathered = lax.all_to_all(compressed, "tower", split_axis=0, concat_axis=1, tiled=True)
    local_rows = gathered.shape[0]
    vector_count = gathered.shape[1] // entry_count
    vectors = gathered.reshape(local_rows, vector_count, entry_count)
    gram_matrix = jnp.einsum(
        "bie,bje->bij", vectors, vectors, preferred_element_type=jnp.float32
    ) * (1.0 / math.sqrt(entry_count))
    pair_terms = gram_matrix.reshape(local_rows, vector_count * vector_count)[
        :, pair_positions(vector_count)
    ]
    joined = jnp.concatenate([dense_vector.astype(jnp.float32), pair_terms], 1).astype(jnp.bfloat16)
    hidden_units = mlp_weight.shape[1]
    hidden_rows = mlp_weight.shape[0]
    tower = lax.axis_index("tower")
    hidden_sum = jnp.zeros((local_rows, hidden_units), jnp.float32)
    for shift, rows in enumerate(hidden_pieces):
        source = (tower - shift) % tower_count
        columns = lax.dynamic_slice_in_dim(joined, source * hidden_rows, hidden_rows, axis=1)
        hidden_sum = hidden_sum + jnp.dot(columns, rows, preferred_element_type=jnp.float32)
    return jax.nn.relu(hidden_sum + mlp_bias[None, :]).astype(jnp.bfloat16)


def solution(mesh):
    in_specs = (
        P("tower", "feat", "groups", None),
        P("tower", "feat", "groups", None),
        P("tower", None),
        P("tower", "feat", None),
        P("tower", "feat", None),
        P("tower", None),
        P("tower", "feat", None),
        P("tower", None),
        P(("groups", "feat", "tower"), None),
        P("tower", None),
        P(),
    )
    out_specs = P(("groups", "feat", "tower"), None)
    body = functools.partial(
        on_device, feat_count=mesh.shape["feat"],
        group_count=mesh.shape["groups"],
        tower_count=mesh.shape["tower"],
    )
    return jax.shard_map(body, mesh=mesh, in_specs=in_specs, out_specs=out_specs, check_vma=False)
```

```python
import functools
import math

import jax
import jax.numpy as jnp
import numpy as np
from jax import lax
from jax.sharding import PartitionSpec as P


def pair_positions(vector_count):
    upper_rows, upper_cols = np.triu_indices(vector_count, 1)
    return upper_rows * vector_count + upper_cols


def weight_parts(weights_here, feat_count, group_count, share_count, entry_count):
    rows_here = weights_here.shape[0]
    piece = rows_here // share_count
    blocks_here = rows_here // entry_count
    blocks_piece = piece // entry_count
    owner = lax.axis_index("feat")
    group = lax.axis_index("groups") if share_count > 1 else 0
    block_range = jnp.arange(blocks_piece, dtype=jnp.int32)
    parts = [(weights_here, owner * blocks_here + jnp.arange(blocks_here, dtype=jnp.int32))]
    if share_count > 1:
        travelling = lax.dynamic_slice_in_dim(weights_here, group * piece, piece, axis=0)
    else:
        travelling = weights_here
    chunk_count = next(count for count in (4, 2, 1) if blocks_piece % count == 0)
    chunk_blocks = blocks_piece // chunk_count
    chunk_rows = chunk_blocks * entry_count
    chunk_range = jnp.arange(chunk_blocks, dtype=jnp.int32)
    rings = [
        lax.slice_in_dim(travelling, chunk * chunk_rows, (chunk + 1) * chunk_rows, axis=0)
        for chunk in range(chunk_count)
    ]
    ring = [(source, (source + 1) % feat_count) for source in range(feat_count)]
    for step in range(1, feat_count):
        source_block = (owner - step) % feat_count
        for chunk in range(chunk_count):
            rings[chunk] = lax.ppermute(rings[chunk], "feat", ring)
            first_block = source_block * blocks_here + chunk * chunk_blocks
            parts.append((rings[chunk], first_block + group * blocks_piece + chunk_range))
            for shift in range(1, share_count):
                pairs = [(source, (source + shift) % group_count) for source in range(group_count)]
                forwarded = lax.ppermute(rings[chunk], "groups", pairs)
                from_group = (group - shift) % group_count
                parts.append((forwarded, first_block + from_group * blocks_piece + chunk_range))
    travelling = rings
    return parts, travelling


def exchange_rows(first, second, feat_count):
    slots_here, row_count, _ = first.shape
    share = row_count // feat_count
    owner = lax.axis_index("feat")
    pieces, ids = [], []
    order = sorted(range(feat_count), key=lambda shift: -min(shift, feat_count - shift))
    for shift in order:
        target = (owner + shift) % feat_count
        piece = jnp.concatenate(
            [
                lax.dynamic_slice_in_dim(first, target * share, share, axis=1),
                lax.dynamic_slice_in_dim(second, target * share, share, axis=1),
            ],
            0,
        )
        if shift:
            piece = lax.ppermute(
                piece, "feat", [(source, (source + shift) % feat_count) for source in range(feat_count)]
            )
        source = (owner - shift) % feat_count
        local = jnp.arange(slots_here, dtype=jnp.int32)
        ids.append(
            jnp.concatenate([source * slots_here + local, (feat_count + source) * slots_here + local])
        )
        pieces.append(piece)
    return pieces, ids


def on_device(
    pooled_first,
    pooled_second,
    feature_order,
    cross_down,
    cross_up,
    cross_bias,
    compress_weight,
    compress_bias,
    dense_vector,
    mlp_weight,
    mlp_bias,
    *,
    feat_count,
    group_count,
    tower_count,
):
    entry_count = pooled_first.shape[3]
    rows_here = cross_down.shape[1]
    rank = cross_down.shape[2]
    split = rows_here % group_count == 0 and (rows_here // group_count) % entry_count == 0
    share_count = group_count if split else 1

    hidden_pieces = [mlp_weight]
    for shift in range(1, tower_count):
        pairs = [(source, (source + shift) % tower_count) for source in range(tower_count)]
        hidden_pieces.append(lax.ppermute(mlp_weight, "tower", pairs))

    weights_here = jnp.concatenate([cross_down[0], cross_up[0], compress_weight[0]], axis=1)
    parts, last_rows = weight_parts(weights_here, feat_count, group_count, share_count, entry_count)

    first_rows, second_rows, _ = lax.optimization_barrier(
        (pooled_first[0], pooled_second[0], last_rows)
    )
    pieces, slot_ids = exchange_rows(first_rows, second_rows, feat_count)
    row_count = pieces[0].shape[1]
    slot_count = sum(piece.shape[0] for piece in pieces)
    bias_blocks = cross_bias[0].reshape(slot_count, entry_count)
    features = jnp.concatenate([part_features for _, part_features in parts])
    position_count = features.shape[0]

    if len(pieces) > 4:
        pieces, slot_ids = [jnp.concatenate(pieces, 0)], [jnp.concatenate(slot_ids)]
    base_sum = None
    for piece, ids in zip(pieces, slot_ids):
        orders = feature_order[0][ids]
        one_hot = (orders[None, :] == features[:, None]).astype(jnp.bfloat16)
        term = jnp.einsum("fs,sre->rfe", one_hot, piece, preferred_element_type=jnp.float32)
        base_sum = term if base_sum is None else base_sum + term
    base_all = base_sum.astype(jnp.bfloat16).reshape(row_count, position_count * entry_count)

    weights = jnp.concatenate([rows for rows, _ in parts], 0)
    low_sum = jnp.dot(base_all, weights[:, :rank], preferred_element_type=jnp.float32)
    low_rank = low_sum.astype(jnp.bfloat16)
    lifted = lax.dot_general(
        low_rank,
        weights[:, rank : 2 * rank],
        (((1,), (1,)), ((), ())),
        preferred_element_type=jnp.float32,
    )
    shift_row = bias_blocks[features].reshape(position_count * entry_count)
    columns = base_all.astype(jnp.float32)
    crossed = (columns * (lifted + shift_row[None, :]) + columns).astype(jnp.bfloat16)
    squeezed = jnp.dot(crossed, weights[:, 2 * rank :], preferred_element_type=jnp.float32)
    compressed = (squeezed + compress_bias[0][None, :]).astype(jnp.bfloat16)
    gathered = lax.all_to_all(compressed, "tower", split_axis=0, concat_axis=1, tiled=True)
    local_rows = gathered.shape[0]
    vector_count = gathered.shape[1] // entry_count
    vectors = gathered.reshape(local_rows, vector_count, entry_count)
    gram_matrix = jnp.einsum(
        "bie,bje->bij", vectors, vectors, preferred_element_type=jnp.float32
    ) * (1.0 / math.sqrt(entry_count))
    pair_terms = gram_matrix.reshape(local_rows, vector_count * vector_count)[
        :, pair_positions(vector_count)
    ]
    joined = jnp.concatenate([dense_vector.astype(jnp.float32), pair_terms], 1).astype(jnp.bfloat16)
    hidden_units = mlp_weight.shape[1]
    hidden_rows = mlp_weight.shape[0]
    tower = lax.axis_index("tower")
    hidden_sum = jnp.zeros((local_rows, hidden_units), jnp.float32)
    for shift, rows in enumerate(hidden_pieces):
        source = (tower - shift) % tower_count
        columns = lax.dynamic_slice_in_dim(joined, source * hidden_rows, hidden_rows, axis=1)
        hidden_sum = hidden_sum + jnp.dot(columns, rows, preferred_element_type=jnp.float32)
    return jax.nn.relu(hidden_sum + mlp_bias[None, :]).astype(jnp.bfloat16)


def solution(mesh):
    in_specs = (
        P("tower", "feat", "groups", None),
        P("tower", "feat", "groups", None),
        P("tower", None),
        P("tower", "feat", None),
        P("tower", "feat", None),
        P("tower", None),
        P("tower", "feat", None),
        P("tower", None),
        P(("groups", "feat", "tower"), None),
        P("tower", None),
        P(),
    )
    out_specs = P(("groups", "feat", "tower"), None)
    body = functools.partial(
        on_device, feat_count=mesh.shape["feat"],
        group_count=mesh.shape["groups"],
        tower_count=mesh.shape["tower"],
    )
    return jax.shard_map(body, mesh=mesh, in_specs=in_specs, out_specs=out_specs, check_vma=False)
```
